512 devices in a mesh: ctx: 32 (over y_hi, z), fsdp: 16 (over y_lo, x, core).
Axes of the slice: x: 4, y: 4 (y_hi: 2, y_lo: 2; y = y_hi * 2 + y_lo), z: 16, core: 2. Of those that a mesh axis runs over, the one named last changes fastest.
Arguments:
- latents: bfloat16 [10240, 3072], P('ctx'), may hold values from -6 to 6, as said below
- timestep: int32 [1], replicated, may hold values from 0 to 999
- offsets: int32 [64], replicated, may hold values from 0 to 63, as said below
- qkv_weight: bfloat16 [3072, 16, 384], P('ctx', 'fsdp'), may hold values from -2 to 2
- mod_weight: bfloat16 [3072, 2, 256], P('ctx'), may hold values from -0.375 to 0.375
- gate_weight: bfloat16 [256, 3072], P(None, 'fsdp'), may hold values from -0.375 to 0.375
- out_weight: bfloat16 [3072, 16, 128], P('ctx', 'fsdp'), may hold values from -0.125 to 0.125
- conv_weight: bfloat16 [3, 3, 3, 3072], P(None, None, None, 'fsdp'), may hold values from -1.25 to 1.25
Outputs:
- mixed: bfloat16 [10240, 3072], P('ctx', 'fsdp')
The draws below stay inside these ranges and needn't reach their ends.
Inputs may be any that keep to these rules, and one draw needn't show every extreme that they name: `latents`: tokens in order of frame, then row, then column. offsets[f] is at most f; the last frame's offset is exactly 63.
All inputs are finite; a program needn't handle non-finite values.
Results may differ from the reference program's by a relative error of at most 0.0095.
Values may be sent and summed in bfloat16 or wider, within the bound.
No kernel may reach another device: no remote copies, remote signals or barrier semaphores. Data moves between devices by JAX's collectives and lax.ppermute only.
A program may use at most 64 MiB of HBM per device.

```python
import math
import jax
import jax.numpy as jnp
from jax import lax

D = 3072
HEADS = 16
DH = 128
TE = 256
HH = 10
WW = 16
TOK_DEV = 320
TOKENS = 10240
FRAMES = 64


def draw_latents(key, part):
    frame_vecs = jax.random.normal(jax.random.fold_in(key, 21), (FRAMES, D), jnp.float32)
    frame_part = jnp.repeat(frame_vecs, HH * WW, axis=0) * 0.7
    noise_rows = jax.random.normal(key, (TOKENS, D), jnp.float32) * 0.7
    return jnp.clip(noise_rows + frame_part, -6.0, 6.0).astype(jnp.bfloat16)


def draw_offsets(key, part):
    raw_values = jax.random.randint(key, (FRAMES,), 0, 1 << 30, dtype=jnp.int32)
    frame_ids = jnp.arange(FRAMES, dtype=jnp.int32)
    drawn = raw_values % (frame_ids + 1)
    return jnp.where(frame_ids == FRAMES - 1, frame_ids, drawn)


def draw_qkv_weight(key, part):
    key_query = jax.random.fold_in(key, 11)
    key_keys = jax.random.fold_in(key, 12)
    key_values = jax.random.fold_in(key, 13)
    shape_one = (D, HEADS, DH)
    query_std = 1.4 / D ** 0.5
    value_std = 1.0 / D ** 0.5
    query_part = jnp.clip(jax.random.normal(key_query, shape_one, jnp.float32), -4.0, 4.0) * query_std
    key_part = jnp.clip(jax.random.normal(key_keys, shape_one, jnp.float32), -4.0, 4.0) * query_std
    value_part = jnp.clip(jax.random.normal(key_values, shape_one, jnp.float32), -4.0, 4.0) * value_std
    return jnp.clip(jnp.concatenate([query_part, key_part, value_part], axis=2), -2.0, 2.0).astype(jnp.bfloat16)


def levels(key, extent, pieces, low, high):
    def one(dim, blocks):
        draws = jax.random.uniform(jax.random.fold_in(jax.random.fold_in(key, 6), dim), (blocks,), jnp.float32, low / len(pieces), high / len(pieces))
        return jnp.repeat(jnp.exp(draws), extent[dim] // blocks).reshape((-1,) + (1,) * (len(extent) - dim - 1))

    loudness = one(*pieces[0])
    for cut in pieces[1:]:
        loudness = loudness * one(*cut)
    return loudness


def bell_draw(key, extent, spread, most, shards=(), kind=jnp.bfloat16):
    values = spread * jax.random.normal(key, extent, jnp.float32)
    if shards:
        values = values * levels(key, extent, shards, -0.22, 0.18)
    return jnp.clip(values, -most, most).astype(kind)


def setup_inputs(seed: int = 0) -> dict:
    seeds = jax.random.split(jax.random.key(seed), 9)
    latents = draw_latents(jax.random.fold_in(seeds[8], 71), 0)
    timestep = jax.random.randint(seeds[1], (1,), 0, 1000).astype(jnp.int32)
    offsets = draw_offsets(jax.random.fold_in(seeds[8], 71), 0)
    qkv_weight = draw_qkv_weight(jax.random.fold_in(seeds[8], 71), 0)
    mod_weight = bell_draw(seeds[4], (D, 2, TE), TE ** -0.5, 0.375, ((0, 32),))
    gate_weight = bell_draw(seeds[5], (TE, D), TE ** -0.5, 0.375, ((1, 16),))
    out_weight = bell_draw(seeds[6], (D, HEADS, DH), (HEADS * DH) ** -0.5, 0.125, ((0, 32), (1, 16)))
    conv_weight = bell_draw(seeds[7], (3, 3, 3, D), 27 ** -0.5, 1.25, ((3, 16),))
    return dict(latents=latents, timestep=timestep, offsets=offsets, qkv_weight=qkv_weight, mod_weight=mod_weight, gate_weight=gate_weight, out_weight=out_weight, conv_weight=conv_weight)


EPS = 1e-06
NEG = -1e+30

def rounded(value):
    return lax.optimization_barrier(value.astype(jnp.bfloat16)).astype(jnp.float32)

def time_features(timestep):
    half_width = TE // 2
    freqs = jnp.exp(-math.log(10000.0) * jnp.arange(half_width, dtype=jnp.float32) / half_width)
    angles = timestep[0].astype(jnp.float32) * freqs
    embed = jnp.concatenate([jnp.cos(angles), jnp.sin(angles)])
    return jax.nn.silu(embed).astype(jnp.bfloat16)

def reference(latents, timestep, offsets, qkv_weight, mod_weight, gate_weight, out_weight, conv_weight):
    time_act = time_features(timestep)
    modulation = jnp.einsum('djt,t->dj', mod_weight.astype(jnp.float32), time_act.astype(jnp.float32))
    gate_vec = jnp.dot(time_act, gate_weight, preferred_element_type=jnp.float32)
    float_rows = latents.astype(jnp.float32)
    centred = float_rows - float_rows.mean(-1, keepdims=True)
    variance = (centred * centred).mean(-1, keepdims=True)
    normed = centred * lax.rsqrt(variance + EPS)
    modulated = rounded(normed * (1.0 + modulation[:, 1]) + modulation[:, 0])
    projected_qkv = rounded(jnp.einsum('nd,dhc->nhc', modulated, qkv_weight.astype(jnp.float32)))
    queries = projected_qkv[:, :, :DH]
    key_part = projected_qkv[:, :, DH:2 * DH]
    value_part = projected_qkv[:, :, 2 * DH:]
    frame_of = jnp.arange(TOKENS, dtype=jnp.int32) // (HH * WW)
    first_seen = offsets[frame_of]
    scale_factor = DH ** (-0.5)

    def one_block(block_no):
        query_rows = lax.dynamic_slice_in_dim(queries, block_no * TOK_DEV, TOK_DEV, 0)
        query_frame = lax.dynamic_slice_in_dim(frame_of, block_no * TOK_DEV, TOK_DEV, 0)
        query_first = lax.dynamic_slice_in_dim(first_seen, block_no * TOK_DEV, TOK_DEV, 0)
        scores = jnp.einsum('nhe,mhe->nhm', query_rows, key_part) * scale_factor
        allowed = (frame_of[None, :] <= query_frame[:, None]) & (frame_of[None, :] >= query_first[:, None])
        masked = jnp.where(allowed[:, None, :], scores, NEG)
        row_top = masked.max(-1, keepdims=True)
        exponent = jnp.where(allowed[:, None, :], jnp.exp(masked - row_top), 0.0)
        row_sum = exponent.sum(-1)
        weights = rounded(exponent)
        summed = jnp.einsum('nhm,mhe->nhe', weights, value_part) / row_sum[..., None]
        return summed.astype(jnp.bfloat16)
    attended = lax.map(one_block, jnp.arange(TOKENS // TOK_DEV, dtype=jnp.int32))
    attended = attended.reshape(TOKENS, HEADS, DH).astype(jnp.float32)
    head_total = jnp.einsum('nhe,dhe->nd', attended, out_weight.astype(jnp.float32))
    grid = float_rows.reshape(FRAMES, HH, WW, D)
    padded = jnp.pad(grid, ((2, 0), (1, 1), (1, 1), (0, 0)))
    convolved = jnp.zeros((FRAMES, HH, WW, D), jnp.float32)
    for time_lag in range(3):
        for row_shift in range(3):
            for col_shift in range(3):
                tap = conv_weight[time_lag, row_shift, col_shift].astype(jnp.float32)
                convolved = convolved + tap * padded[2 - time_lag:2 - time_lag + FRAMES, row_shift:row_shift + HH, col_shift:col_shift + WW]
    mixed = float_rows + gate_vec * head_total + convolved.reshape(TOKENS, D)
    return mixed.astype(jnp.bfloat16)
```

```python
import math

import jax
import jax.numpy as jnp
from jax import lax
from jax.sharding import PartitionSpec as P

HH = 10
WW = 16


EPS = 1e-06
NEG = -1e30


def passed_along(block, axis, distance):
    devices = range(lax.axis_size(axis))
    route = [(i - distance, i) for i in devices if i - distance in devices]
    return lax.ppermute(block, axis, route)


def time_features(timestep, embed_width):
    half_width = embed_width // 2
    freqs = jnp.exp(-math.log(10000.0) * jnp.arange(half_width, dtype=jnp.float32) / half_width)
    angles = timestep[0].astype(jnp.float32) * freqs
    embed = jnp.concatenate([jnp.cos(angles), jnp.sin(angles)])
    return jax.nn.silu(embed).astype(jnp.bfloat16)


def attend_piece(
    state_now, kv_piece, first_key, queries, query_frame, query_first, frame_size, head_dim
):
    run_max, run_sum, accumulated = state_now
    key_count = kv_piece.shape[0]
    key_part = kv_piece[:, :, :head_dim]
    value_part = kv_piece[:, :, head_dim:]
    scores = jnp.einsum(
        "nhe,mhe->nhm", queries, key_part, preferred_element_type=jnp.float32
    ) * head_dim ** (-0.5)
    key_frame = (first_key + jnp.arange(key_count, dtype=jnp.int32)) // frame_size
    allowed = (key_frame[None, :] <= query_frame[:, None]) & (
        key_frame[None, :] >= query_first[:, None]
    )
    masked = jnp.where(allowed[:, None, :], scores, NEG)
    new_max = jnp.maximum(run_max, masked.max(-1))
    exponent = jnp.where(allowed[:, None, :], jnp.exp(masked - new_max[..., None]), 0.0)
    factor = jnp.exp(run_max - new_max)
    run_sum = run_sum * factor + exponent.sum(-1)
    accumulated = accumulated * factor[..., None] + jnp.einsum(
        "nhm,mhe->nhe",
        exponent.astype(jnp.bfloat16),
        value_part,
        preferred_element_type=jnp.float32,
    )
    return (new_max, run_sum, accumulated)


def fold_blocks(state_now, kv_piece, step_fn, block_rows):
    key_count = kv_piece.shape[0]
    split_rows = kv_piece.reshape(
        key_count // block_rows, block_rows, kv_piece.shape[1], kv_piece.shape[2]
    )

    def visit_block(state_in, block_item):
        block_no, block_rows_kv = block_item
        return (step_fn(state_in, block_rows_kv, block_no * block_rows), None)

    block_ids = jnp.arange(key_count // block_rows, dtype=jnp.int32)
    state_out, _ = lax.scan(visit_block, state_now, (block_ids, split_rows))
    return state_out


def per_device(
    latents, timestep, offsets, qkv_weight, mod_weight, gate_weight, out_weight, conv_weight
):
    tok_rows = latents.shape[0]
    heads_here = qkv_weight.shape[1]
    head_dim = out_weight.shape[2]
    chan_here = gate_weight.shape[1]
    frame_size = HH * WW
    frames_here = tok_rows // frame_size
    position = lax.axis_index("ctx")
    column = lax.axis_index("fsdp")
    time_act = time_features(timestep, gate_weight.shape[0])
    gate_vec = jnp.dot(time_act, gate_weight, preferred_element_type=jnp.float32)
    float_rows = latents.astype(jnp.float32)
    centred = float_rows - float_rows.mean(-1, keepdims=True)
    variance = (centred * centred).mean(-1, keepdims=True)
    normed = centred * lax.rsqrt(variance + EPS)
    rows_here = qkv_weight.shape[0]
    qkv_width = qkv_weight.shape[2]
    local_shares = jnp.einsum(
        "rjt,t->rj", mod_weight, time_act, preferred_element_type=jnp.float32
    )
    shares_hi = local_shares.astype(jnp.bfloat16)
    shares_lo = (local_shares - shares_hi.astype(jnp.float32)).astype(jnp.bfloat16)
    bundle = jnp.concatenate(
        [
            qkv_weight.reshape(rows_here, heads_here * qkv_width),
            out_weight.reshape(rows_here, heads_here * head_dim),
            shares_hi,
            shares_lo,
        ],
        axis=1,
    )
    gathered = lax.all_gather(bundle, "ctx", axis=0, tiled=True)
    full_rows = gathered.shape[0]
    qkv_cols = heads_here * qkv_width
    out_cols = heads_here * head_dim
    w_piece = gathered[:, :qkv_cols].reshape(full_rows, heads_here, qkv_width)
    o_piece = gathered[:, qkv_cols : qkv_cols + out_cols].reshape(full_rows, heads_here, head_dim)
    share_bits = gathered[:, qkv_cols + out_cols :].astype(jnp.float32)
    shares = share_bits[:, :2] + share_bits[:, 2:]
    modulated = (normed * (1.0 + shares[:, 1]) + shares[:, 0]).astype(jnp.bfloat16)
    projected_qkv = jnp.einsum(
        "nr,rhc->nhc", modulated, w_piece, preferred_element_type=jnp.float32
    ).astype(jnp.bfloat16)
    queries = projected_qkv[:, :, :head_dim]
    packed = projected_qkv[:, :, head_dim:]
    query_frame = position * frames_here + jnp.arange(tok_rows, dtype=jnp.int32) // frame_size
    local_first = lax.dynamic_slice_in_dim(offsets, position * frames_here, frames_here, 0)
    query_first = jnp.repeat(local_first, frame_size)
    start_state = (
        jnp.full((tok_rows, heads_here), NEG, jnp.float32),
        jnp.zeros((tok_rows, heads_here), jnp.float32),
        jnp.zeros((tok_rows, heads_here, head_dim), jnp.float32),
    )
    block_rows = 2 * tok_rows

    def attend(state_now, kv_piece, first_key):
        return attend_piece(
            state_now, kv_piece, first_key, queries, query_frame, query_first, frame_size, head_dim
        )

    run_max, run_sum, accumulated = fold_blocks(
        start_state, lax.all_gather(packed, "ctx", axis=0, tiled=True), attend, block_rows
    )
    attended = (accumulated / run_sum[..., None]).astype(jnp.bfloat16)
    partial_out = jnp.einsum(
        "nhe,rhe->nr",
        attended,
        o_piece,
        preferred_element_type=jnp.float32,
    )
    head_total = lax.psum_scatter(
        partial_out.astype(jnp.bfloat16), "fsdp", scatter_dimension=1, tiled=True
    ).astype(jnp.float32)
    own_chan = lax.dynamic_slice_in_dim(latents, column * chan_here, chan_here, 1)
    before = passed_along(own_chan, "ctx", 1)
    stacked = (
        jnp.concatenate([before, own_chan], 0)
        .astype(jnp.float32)
        .reshape(frames_here + 2, HH, WW, chan_here)
    )
    padded = jnp.pad(stacked, ((0, 0), (1, 1), (1, 1), (0, 0)))
    convolved = jnp.zeros((frames_here, HH, WW, chan_here), jnp.float32)
    for time_lag in range(3):
        for row_shift in range(3):
            for col_shift in range(3):
                tap = conv_weight[time_lag, row_shift, col_shift].astype(jnp.float32)
                convolved = (
                    convolved
                    + tap
                    * padded[
                        2 - time_lag : 2 - time_lag + frames_here,
                        row_shift : row_shift + HH,
                        col_shift : col_shift + WW,
                    ]
                )
    residual = own_chan.astype(jnp.float32)
    mixed = residual + gate_vec * head_total + convolved.reshape(tok_rows, chan_here)
    return mixed.astype(jnp.bfloat16)


def solution(mesh):
    in_specs = (
        P("ctx", None),
        P(),
        P(),
        P("ctx", "fsdp", None),
        P("ctx", None, None),
        P(None, "fsdp"),
        P("ctx", "fsdp", None),
        P(None, None, None, "fsdp"),
    )
    out_specs = P("ctx", "fsdp")
    return jax.shard_map(
        per_device, mesh=mesh, in_specs=in_specs, out_specs=out_specs, check_vma=False
    )
```

```python
import math

import jax
import jax.numpy as jnp
from jax import lax
from jax.sharding import PartitionSpec as P

HH = 10
WW = 16


EPS = 1e-06
NEG = -1e30


def passed_along(block, axis, distance):
    devices = range(lax.axis_size(axis))
    route = [(i - distance, i) for i in devices if i - distance in devices]
    return lax.ppermute(block, axis, route)


def time_features(timestep, embed_width):
    half_width = embed_width // 2
    freqs = jnp.exp(-math.log(10000.0) * jnp.arange(half_width, dtype=jnp.float32) / half_width)
    angles = timestep[0].astype(jnp.float32) * freqs
    embed = jnp.concatenate([jnp.cos(angles), jnp.sin(angles)])
    return jax.nn.silu(embed).astype(jnp.bfloat16)


def ring_pieces(block, axis):
    size = lax.axis_size(axis)
    ring = size // 2
    position = lax.axis_index(axis)
    partner = lax.ppermute(block, axis, [(i, (i + ring) % size) for i in range(size)])
    pair = jnp.where(
        position // ring == 0, jnp.stack([block, partner]), jnp.stack([partner, block])
    )
    ring_pos = position % ring
    forward = [(y * ring + a, y * ring + (a + 1) % ring) for y in range(2) for a in range(ring)]
    backward = [(y * ring + a, y * ring + (a - 1) % ring) for y in range(2) for a in range(ring)]
    pieces = [(pair, ring_pos)]
    ahead = pair
    behind = pair
    for step in range(1, ring // 2 + 1):
        ahead = lax.ppermute(ahead, axis, forward)
        pieces.append((ahead, (ring_pos - step) % ring))
        if step < ring - ring // 2:
            behind = lax.ppermute(behind, axis, backward)
            pieces.append((behind, (ring_pos + step) % ring))
    return pieces, ring


def ring_gather(block, axis):
    pieces, ring = ring_pieces(block, axis)
    gathered = jnp.zeros((ring,) + pieces[0][0].shape, block.dtype)
    for piece, source in pieces:
        gathered = lax.dynamic_update_index_in_dim(gathered, piece, source, 0)
    gathered = jnp.swapaxes(gathered, 0, 1)
    return gathered.reshape((2 * ring * block.shape[0],) + block.shape[1:])


def halving_scatter(partial, axis):
    size = lax.axis_size(axis)
    bits = size.bit_length() - 1
    position = lax.axis_index(axis)
    rows, cols = partial.shape
    width = cols // size
    state = partial.reshape((rows,) + (2,) * bits + (width,))
    axis_bits = [bits - 1 - a for a in range(bits)]
    order = [0] + ([bits - 1] if bits > 1 else []) + list(range(1, bits - 1))
    for bit in order:
        dim = 1 + axis_bits.index(bit)
        mine = (position >> bit) & 1
        low = lax.index_in_dim(state, 0, dim, keepdims=False)
        high = lax.index_in_dim(state, 1, dim, keepdims=False)
        keep = jnp.where(mine == 0, low, high)
        send = jnp.where(mine == 0, high, low)
        got = lax.ppermute(
            send.astype(jnp.bfloat16), axis, [(i, i ^ (1 << bit)) for i in range(size)]
        )
        state = keep + got.astype(jnp.float32)
        axis_bits.remove(bit)
    return state.reshape(rows, width)


def attend_piece(state_now, kv_piece, key_frame, queries, query_frame, query_first, head_dim):
    run_max, run_sum, accumulated = state_now
    key_part = kv_piece[:, :, :head_dim]
    value_part = kv_piece[:, :, head_dim:]
    scores = jnp.einsum(
        "nhe,mhe->nhm", queries, key_part, preferred_element_type=jnp.float32
    ) * head_dim ** (-0.5)
    allowed = (key_frame[None, :] <= query_frame[:, None]) & (
        key_frame[None, :] >= query_first[:, None]
    )
    masked = jnp.where(allowed[:, None, :], scores, NEG)
    new_max = jnp.maximum(run_max, masked.max(-1))
    exponent = jnp.where(allowed[:, None, :], jnp.exp(masked - new_max[..., None]), 0.0)
    factor = jnp.exp(run_max - new_max)
    run_sum = run_sum * factor + exponent.sum(-1)
    accumulated = accumulated * factor[..., None] + jnp.einsum(
        "nhm,mhe->nhe",
        exponent.astype(jnp.bfloat16),
        value_part,
        preferred_element_type=jnp.float32,
    )
    return (new_max, run_sum, accumulated)


def per_device(
    latents, timestep, offsets, qkv_weight, mod_weight, gate_weight, out_weight, conv_weight
):
    tok_rows = latents.shape[0]
    heads_here = qkv_weight.shape[1]
    head_dim = out_weight.shape[2]
    chan_here = gate_weight.shape[1]
    frame_size = HH * WW
    frames_here = tok_rows // frame_size
    position = lax.axis_index("ctx")
    column = lax.axis_index("fsdp")
    time_act = time_features(timestep, gate_weight.shape[0])
    gate_vec = jnp.dot(time_act, gate_weight, preferred_element_type=jnp.float32)
    float_rows = latents.astype(jnp.float32)
    centred = float_rows - float_rows.mean(-1, keepdims=True)
    variance = (centred * centred).mean(-1, keepdims=True)
    normed = centred * lax.rsqrt(variance + EPS)

    rows_here = qkv_weight.shape[0]
    qkv_width = qkv_weight.shape[2]
    qkv_cols = heads_here * qkv_width
    out_cols = heads_here * head_dim
    width = qkv_cols + out_cols
    local_shares = jnp.einsum(
        "rjt,t->rj", mod_weight, time_act, preferred_element_type=jnp.float32
    )
    shares_hi = local_shares.astype(jnp.bfloat16)
    shares_lo = (local_shares - shares_hi.astype(jnp.float32)).astype(jnp.bfloat16)
    share_count = 4 * rows_here
    extra_rows = 16 * ((share_count + 16 * width - 1) // (16 * width))
    share_block = jnp.zeros((extra_rows * width,), jnp.bfloat16)
    share_block = share_block.at[:share_count].set(
        jnp.concatenate([shares_hi, shares_lo], axis=1).reshape(share_count)
    )
    bundle = jnp.concatenate(
        [
            jnp.concatenate(
                [
                    qkv_weight.reshape(rows_here, qkv_cols),
                    out_weight.reshape(rows_here, out_cols),
                ],
                axis=1,
            ),
            share_block.reshape(extra_rows, width),
        ],
        axis=0,
    )
    gathered = ring_gather(bundle, "ctx")
    blocks = gathered.shape[0] // bundle.shape[0]
    gathered = gathered.reshape(blocks, rows_here + extra_rows, width)
    full_rows = blocks * rows_here
    w_piece = gathered[:, :rows_here, :qkv_cols].reshape(full_rows, heads_here, qkv_width)
    o_piece = gathered[:, :rows_here, qkv_cols:].reshape(full_rows, heads_here, head_dim)
    share_bits = (
        gathered[:, rows_here:, :]
        .reshape(blocks, extra_rows * width)[:, :share_count]
        .reshape(full_rows, 4)
        .astype(jnp.float32)
    )
    shares = share_bits[:, :2] + share_bits[:, 2:]

    modulated = (normed * (1.0 + shares[:, 1]) + shares[:, 0]).astype(jnp.bfloat16)
    projected_qkv = jnp.einsum(
        "nr,rhc->nhc", modulated, w_piece, preferred_element_type=jnp.float32
    ).astype(jnp.bfloat16)
    queries = projected_qkv[:, :, :head_dim]
    packed = projected_qkv[:, :, head_dim:]
    query_frame = position * frames_here + jnp.arange(tok_rows, dtype=jnp.int32) // frame_size
    local_first = lax.dynamic_slice_in_dim(offsets, position * frames_here, frames_here, 0)
    query_first = jnp.repeat(local_first, frame_size)
    state = (
        jnp.full((tok_rows, heads_here), NEG, jnp.float32),
        jnp.zeros((tok_rows, heads_here), jnp.float32),
        jnp.zeros((tok_rows, heads_here, head_dim), jnp.float32),
    )
    kv_pieces, ring = ring_pieces(packed, "ctx")
    token_ids = jnp.arange(tok_rows, dtype=jnp.int32)
    for piece, source in kv_pieces:
        key_frame = (
            jnp.concatenate(
                [source * tok_rows + token_ids, (ring + source) * tok_rows + token_ids]
            )
            // frame_size
        )
        state = attend_piece(
            state,
            piece.reshape((2 * tok_rows,) + piece.shape[2:]),
            key_frame,
            queries,
            query_frame,
            query_first,
            head_dim,
        )
    run_max, run_sum, accumulated = state
    attended = (accumulated / run_sum[..., None]).astype(jnp.bfloat16)
    partial_out = jnp.einsum(
        "nhe,rhe->nr",
        attended,
        o_piece,
        preferred_element_type=jnp.float32,
    )
    head_total = halving_scatter(partial_out, "fsdp")
    own_chan = lax.dynamic_slice_in_dim(latents, column * chan_here, chan_here, 1)
    before = passed_along(own_chan, "ctx", 1)
    stacked = (
        jnp.concatenate([before, own_chan], 0)
        .astype(jnp.float32)
        .reshape(frames_here + 2, HH, WW, chan_here)
    )
    padded = jnp.pad(stacked, ((0, 0), (1, 1), (1, 1), (0, 0)))
    convolved = jnp.zeros((frames_here, HH, WW, chan_here), jnp.float32)
    for time_lag in range(3):
        for row_shift in range(3):
            for col_shift in range(3):
                tap = conv_weight[time_lag, row_shift, col_shift].astype(jnp.float32)
                convolved = (
                    convolved
                    + tap
                    * padded[
                        2 - time_lag : 2 - time_lag + frames_here,
                        row_shift : row_shift + HH,
                        col_shift : col_shift + WW,
                    ]
                )
    residual = own_chan.astype(jnp.float32)
    mixed = residual + gate_vec * head_total + convolved.reshape(tok_rows, chan_here)
    return mixed.astype(jnp.bfloat16)


def solution(mesh):
    in_specs = (
        P("ctx", None),
        P(),
        P(),
        P("ctx", "fsdp", None),
        P("ctx", None, None),
        P(None, "fsdp"),
        P("ctx", "fsdp", None),
        P(None, None, None, "fsdp"),
    )
    out_specs = P("ctx", "fsdp")
    return jax.shard_map(
        per_device, mesh=mesh, in_specs=in_specs, out_specs=out_specs, check_vma=False
    )
```

```python
import math

import jax
import jax.numpy as jnp
from jax import lax
from jax.sharding import PartitionSpec as P

HH = 10
WW = 16


EPS = 1e-06
NEG = -1e30


def passed_along(block, axis, distance):
    devices = range(lax.axis_size(axis))
    route = [(i - distance, i) for i in devices if i - distance in devices]
    return lax.ppermute(block, axis, route)


def time_features(timestep, embed_width):
    half_width = embed_width // 2
    freqs = jnp.exp(-math.log(10000.0) * jnp.arange(half_width, dtype=jnp.float32) / half_width)
    angles = timestep[0].astype(jnp.float32) * freqs
    embed = jnp.concatenate([jnp.cos(angles), jnp.sin(angles)])
    return jax.nn.silu(embed).astype(jnp.bfloat16)


def ring_pieces(block, axis):
    size = lax.axis_size(axis)
    ring = size // 2
    position = lax.axis_index(axis)
    partner = lax.ppermute(block, axis, [(i, (i + ring) % size) for i in range(size)])
    pair = jnp.where(
        position // ring == 0, jnp.stack([block, partner]), jnp.stack([partner, block])
    )
    ring_pos = position % ring
    forward = [(y * ring + a, y * ring + (a + 1) % ring) for y in range(2) for a in range(ring)]
    backward = [(y * ring + a, y * ring + (a - 1) % ring) for y in range(2) for a in range(ring)]
    pieces = [(pair, ring_pos)]
    ahead = pair
    behind = pair
    for step in range(1, ring // 2 + 1):
        ahead = lax.ppermute(ahead, axis, forward)
        pieces.append((ahead, (ring_pos - step) % ring))
        if step < ring - ring // 2:
            behind = lax.ppermute(behind, axis, backward)
            pieces.append((behind, (ring_pos + step) % ring))
    return pieces, ring


def ring_gather(block, axis):
    pieces, ring = ring_pieces(block, axis)
    gathered = jnp.zeros((ring,) + pieces[0][0].shape, block.dtype)
    for piece, source in pieces:
        gathered = lax.dynamic_update_index_in_dim(gathered, piece, source, 0)
    gathered = jnp.swapaxes(gathered, 0, 1)
    return gathered.reshape((2 * ring * block.shape[0],) + block.shape[1:])


def block_order(size, order):
    bits = len(order)
    return [
        sum(((j >> order[s]) & 1) << (bits - 1 - s) for s in range(bits)) for j in range(size)
    ]


def halving_scatter(partial, axis, order):
    size = lax.axis_size(axis)
    position = lax.axis_index(axis)
    state = partial
    for bit in order:
        half = state.shape[1] // 2
        mine = (position >> bit) & 1
        keep = lax.dynamic_slice_in_dim(state, mine * half, half, 1)
        send = lax.dynamic_slice_in_dim(state, (1 - mine) * half, half, 1)
        got = lax.ppermute(
            send.astype(jnp.bfloat16), axis, [(i, i ^ (1 << bit)) for i in range(size)]
        )
        state = keep + got.astype(jnp.float32)
    return state


def attend_piece(state_now, kv_piece, key_frame, queries, query_frame, query_first, head_dim):
    run_max, run_sum, accumulated = state_now
    key_part = kv_piece[:, :, :head_dim]
    value_part = kv_piece[:, :, head_dim:]
    scores = jnp.einsum(
        "nhe,mhe->nhm", queries, key_part, preferred_element_type=jnp.float32
    ) * head_dim ** (-0.5)
    allowed = (key_frame[None, :] <= query_frame[:, None]) & (
        key_frame[None, :] >= query_first[:, None]
    )
    masked = jnp.where(allowed[:, None, :], scores, NEG)
    new_max = jnp.maximum(run_max, masked.max(-1))
    exponent = jnp.where(allowed[:, None, :], jnp.exp(masked - new_max[..., None]), 0.0)
    factor = jnp.exp(run_max - new_max)
    run_sum = run_sum * factor + exponent.sum(-1)
    accumulated = accumulated * factor[..., None] + jnp.einsum(
        "nhm,mhe->nhe",
        exponent.astype(jnp.bfloat16),
        value_part,
        preferred_element_type=jnp.float32,
    )
    return (new_max, run_sum, accumulated)


def per_device(
    latents, timestep, offsets, qkv_weight, mod_weight, gate_weight, out_weight, conv_weight
):
    tok_rows = latents.shape[0]
    heads_here = qkv_weight.shape[1]
    head_dim = out_weight.shape[2]
    chan_here = gate_weight.shape[1]
    frame_size = HH * WW
    frames_here = tok_rows // frame_size
    position = lax.axis_index("ctx")
    column = lax.axis_index("fsdp")
    time_act = time_features(timestep, gate_weight.shape[0])
    gate_vec = jnp.dot(time_act, gate_weight, preferred_element_type=jnp.float32)
    float_rows = latents.astype(jnp.float32)
    centred = float_rows - float_rows.mean(-1, keepdims=True)
    variance = (centred * centred).mean(-1, keepdims=True)
    normed = centred * lax.rsqrt(variance + EPS)

    rows_here = qkv_weight.shape[0]
    qkv_width = qkv_weight.shape[2]
    qkv_cols = heads_here * qkv_width
    out_cols = heads_here * head_dim
    width = qkv_cols + out_cols
    local_shares = jnp.einsum(
        "rjt,t->rj", mod_weight, time_act, preferred_element_type=jnp.float32
    )
    shares_hi = local_shares.astype(jnp.bfloat16)
    shares_lo = (local_shares - shares_hi.astype(jnp.float32)).astype(jnp.bfloat16)
    share_count = 4 * rows_here
    extra_rows = 16 * ((share_count + 16 * width - 1) // (16 * width))
    share_block = jnp.zeros((extra_rows * width,), jnp.bfloat16)
    share_block = share_block.at[:share_count].set(
        jnp.concatenate([shares_hi, shares_lo], axis=1).reshape(share_count)
    )
    bundle = jnp.concatenate(
        [
            jnp.concatenate(
                [
                    qkv_weight.reshape(rows_here, qkv_cols),
                    out_weight.reshape(rows_here, out_cols),
                ],
                axis=1,
            ),
            share_block.reshape(extra_rows, width),
        ],
        axis=0,
    )
    gathered = ring_gather(bundle, "ctx")
    blocks = gathered.shape[0] // bundle.shape[0]
    gathered = gathered.reshape(blocks, rows_here + extra_rows, width)
    full_rows = blocks * rows_here
    w_piece = gathered[:, :rows_here, :qkv_cols].reshape(full_rows, heads_here, qkv_width)
    o_piece = gathered[:, :rows_here, qkv_cols:].reshape(full_rows, heads_here, head_dim)
    share_bits = (
        gathered[:, rows_here:, :]
        .reshape(blocks, extra_rows * width)[:, :share_count]
        .reshape(full_rows, 4)
        .astype(jnp.float32)
    )
    shares = share_bits[:, :2] + share_bits[:, 2:]

    modulated = (normed * (1.0 + shares[:, 1]) + shares[:, 0]).astype(jnp.bfloat16)
    projected_qkv = jnp.einsum(
        "nr,rhc->nhc", modulated, w_piece, preferred_element_type=jnp.float32
    ).astype(jnp.bfloat16)
    queries = projected_qkv[:, :, :head_dim]
    packed = projected_qkv[:, :, head_dim:]
    query_frame = position * frames_here + jnp.arange(tok_rows, dtype=jnp.int32) // frame_size
    local_first = lax.dynamic_slice_in_dim(offsets, position * frames_here, frames_here, 0)
    query_first = jnp.repeat(local_first, frame_size)
    state = (
        jnp.full((tok_rows, heads_here), NEG, jnp.float32),
        jnp.zeros((tok_rows, heads_here), jnp.float32),
        jnp.zeros((tok_rows, heads_here, head_dim), jnp.float32),
    )
    kv_pieces, ring = ring_pieces(packed, "ctx")
    token_ids = jnp.arange(tok_rows, dtype=jnp.int32)
    for piece, source in kv_pieces:
        key_frame = (
            jnp.concatenate(
                [source * tok_rows + token_ids, (ring + source) * tok_rows + token_ids]
            )
            // frame_size
        )
        state = attend_piece(
            state,
            piece.reshape((2 * tok_rows,) + piece.shape[2:]),
            key_frame,
            queries,
            query_frame,
            query_first,
            head_dim,
        )
    run_max, run_sum, accumulated = state_now
    key_part = kv_piece[:, :, :head_dim]
    value_part = kv_piece[:, :, head_dim:]
    scores = jnp.einsum(
        "nhe,mhe->nhm", queries, key_part, preferred_element_type=jnp.float32
    ) * head_dim ** (-0.5)
    allowed = (key_frame[None, :] <= query_frame[:, None]) & (
        key_frame[None, :] >= query_first[:, None]
    )
    masked = jnp.where(allowed[:, None, :], scores, NEG)
    new_max = jnp.maximum(run_max, masked.max(-1))
    exponent = jnp.where(allowed[:, None, :], jnp.exp(masked - new_max[..., None]), 0.0)
    factor = jnp.exp(run_max - new_max)
    run_sum = run_sum * factor + exponent.sum(-1)
    accumulated = accumulated * factor[..., None] + jnp.einsum(
        "nhm,mhe->nhe",
        exponent.astype(jnp.bfloat16),
        value_part,
        preferred_element_type=jnp.float32,
    )
    return (new_max, run_sum, accumulated)


def per_device(
    latents, timestep, offsets, qkv_weight, mod_weight, gate_weight, out_weight, conv_weight
):
    tok_rows = latents.shape[0]
    heads_here = qkv_weight.shape[1]
    head_dim = out_weight.shape[2]
    chan_here = gate_weight.shape[1]
    frame_size = HH * WW
    frames_here = tok_rows // frame_size
    position = lax.axis_index("ctx")
    column = lax.axis_index("fsdp")
    time_act = time_features(timestep, gate_weight.shape[0])
    gate_vec = jnp.dot(time_act, gate_weight, preferred_element_type=jnp.float32)
    float_rows = latents.astype(jnp.float32)
    centred = float_rows - float_rows.mean(-1, keepdims=True)
    variance = (centred * centred).mean(-1, keepdims=True)
    normed = centred * lax.rsqrt(variance + EPS)

    rows_here = qkv_weight.shape[0]
    qkv_width = qkv_weight.shape[2]
    qkv_cols = heads_here * qkv_width
    out_cols = heads_here * head_dim
    width = qkv_cols + out_cols
    local_shares = jnp.einsum(
        "rjt,t->rj", mod_weight, time_act, preferred_element_type=jnp.float32
    )
    shares_hi = local_shares.astype(jnp.bfloat16)
    shares_lo = (local_shares - shares_hi.astype(jnp.float32)).astype(jnp.bfloat16)
    share_count = 4 * rows_here
    extra_rows = 16 * ((share_count + 16 * width - 1) // (16 * width))
    share_block = jnp.zeros((extra_rows * width,), jnp.bfloat16)
    share_block = share_block.at[:share_count].set(
        jnp.concatenate([shares_hi, shares_lo], axis=1).reshape(share_count)
    )
    bundle = jnp.concatenate(
        [
            jnp.concatenate(
                [
                    qkv_weight.reshape(rows_here, qkv_cols),
                    out_weight.reshape(rows_here, out_cols),
                ],
                axis=1,
            ),
            share_block.reshape(extra_rows, width),
        ],
        axis=0,
    )
    gathered = ring_gather(bundle, "ctx")
    blocks = gathered.shape[0] // bundle.shape[0]
    gathered = gathered.reshape(blocks, rows_here + extra_rows, width)
    full_rows = blocks * rows_here
    w_piece = gathered[:, :rows_here, :qkv_cols].reshape(full_rows, heads_here, qkv_width)
    o_piece = gathered[:, :rows_here, qkv_cols:].reshape(full_rows, heads_here, head_dim)
    share_bits = (
        gathered[:, rows_here:, :]
        .reshape(blocks, extra_rows * width)[:, :share_count]
        .reshape(full_rows, 4)
        .astype(jnp.float32)
    )
    shares = share_bits[:, :2] + share_bits[:, 2:]

    modulated = (normed * (1.0 + shares[:, 1]) + shares[:, 0]).astype(jnp.bfloat16)
    projected_qkv = jnp.einsum(
        "nr,rhc->nhc", modulated, w_piece, preferred_element_type=jnp.float32
    ).astype(jnp.bfloat16)
    queries = projected_qkv[:, :, :head_dim]
    packed = projected_qkv[:, :, head_dim:]
    query_frame = position * frames_here + jnp.arange(tok_rows, dtype=jnp.int32) // frame_size
    local_first = lax.dynamic_slice_in_dim(offsets, position * frames_here, frames_here, 0)
    query_first = jnp.repeat(local_first, frame_size)
    state = (
        jnp.full((tok_rows, heads_here), NEG, jnp.float32),
        jnp.zeros((tok_rows, heads_here), jnp.float32),
        jnp.zeros((tok_rows, heads_here, head_dim), jnp.float32),
    )
    kv_pieces, ring = ring_pieces(packed, "ctx")
    token_ids = jnp.arange(tok_rows, dtype=jnp.int32)
    step_groups = [kv_pieces[:1]] + [
        kv_pieces[i : i + 2] for i in range(1, len(kv_pieces), 2)
    ]
    for group in step_groups:
        key_frame = (
            jnp.concatenate(
                [
                    jnp.concatenate(
                        [source * tok_rows + token_ids, (ring + source) * tok_rows + token_ids]
                    )
                    for _, source in group
                ]
            )
            // frame_size
        )
        keys_values = jnp.concatenate(
            [piece.reshape((2 * tok_rows,) + piece.shape[2:]) for piece, _ in group]
        )
        state = attend_piece(
            state, keys_values, key_frame, queries, query_frame, query_first, head_dim
        )
    run_max, run_sum, accumulated = state
    attended = (accumulated / run_sum[..., None]).astype(jnp.bfloat16)
    size = lax.axis_size("fsdp")
    bits = size.bit_length() - 1
    middle = list(range(1, bits - 1))
    half_rows = tok_rows // 2
    orders = [[0, bits - 1] + middle, [0] + middle + [bits - 1]]
    head_parts = []
    for part, order in enumerate(orders):
        positions = block_order(size, order)
        by_block = o_piece.reshape((size, full_rows // size) + o_piece.shape[1:])
        permuted = jnp.stack([by_block[positions.index(q)] for q in range(size)])
        partial_out = jnp.einsum(
            "nhe,rhe->nr",
            attended[part * half_rows : (part + 1) * half_rows],
            permuted.reshape(o_piece.shape),
            preferred_element_type=jnp.float32,
        )
        head_parts.append(halving_scatter(partial_out, "fsdp", order))
    head_total = jnp.concatenate(head_parts, axis=0)
    own_chan = lax.dynamic_slice_in_dim(latents, column * chan_here, chan_here, 1)
    before = passed_along(own_chan, "ctx", 1)
    stacked = (
        jnp.concatenate([before, own_chan], 0)
        .astype(jnp.float32)
        .reshape(frames_here + 2, HH, WW, chan_here)
    )
    padded = jnp.pad(stacked, ((0, 0), (1, 1), (1, 1), (0, 0)))
    convolved = jnp.zeros((frames_here, HH, WW, chan_here), jnp.float32)
    for time_lag in range(3):
        for row_shift in range(3):
            for col_shift in range(3):
                tap = conv_weight[time_lag, row_shift, col_shift].astype(jnp.float32)
                convolved = (
                    convolved
                    + tap
                    * padded[
                        2 - time_lag : 2 - time_lag + frames_here,
                        row_shift : row_shift + HH,
                        col_shift : col_shift + WW,
                    ]
                )
    residual = own_chan.astype(jnp.float32)
    mixed = residual + gate_vec * head_total + convolved.reshape(tok_rows, chan_here)
    return mixed.astype(jnp.bfloat16)


def solution(mesh):
    in_specs = (
        P("ctx", None),
        P(),
        P(),
        P("ctx", "fsdp", None),
        P("ctx", None, None),
        P(None, "fsdp"),
        P("ctx", "fsdp", None),
        P(None, None, None, "fsdp"),
    )
    out_specs = P("ctx", "fsdp")
    return jax.shard_map(
        per_device, mesh=mesh, in_specs=in_specs, out_specs=out_specs, check_vma=False
    )
```

```python
import math

import jax
import jax.numpy as jnp
from jax import lax
from jax.sharding import PartitionSpec as P

HH = 10
WW = 16


EPS = 1e-06
NEG = -1e30


def passed_along(block, axis, distance):
    devices = range(lax.axis_size(axis))
    route = [(i - distance, i) for i in devices if i - distance in devices]
    return lax.ppermute(block, axis, route)


def time_features(timestep, embed_width):
    half_width = embed_width // 2
    freqs = jnp.exp(-math.log(10000.0) * jnp.arange(half_width, dtype=jnp.float32) / half_width)
    angles = timestep[0].astype(jnp.float32) * freqs
    embed = jnp.concatenate([jnp.cos(angles), jnp.sin(angles)])
    return jax.nn.silu(embed).astype(jnp.bfloat16)


def ring_pieces(block, axis):
    size = lax.axis_size(axis)
    ring = size // 2
    position = lax.axis_index(axis)
    partner = lax.ppermute(block, axis, [(i, (i + ring) % size) for i in range(size)])
    pair = jnp.where(
        position // ring == 0, jnp.stack([block, partner]), jnp.stack([partner, block])
    )
    ring_pos = position % ring
    forward = [(y * ring + a, y * ring + (a + 1) % ring) for y in range(2) for a in range(ring)]
    backward = [(y * ring + a, y * ring + (a - 1) % ring) for y in range(2) for a in range(ring)]
    pieces = [(pair, ring_pos)]
    ahead = pair
    behind = pair
    for step in range(1, ring // 2 + 1):
        ahead = lax.ppermute(ahead, axis, forward)
        pieces.append((ahead, (ring_pos - step) % ring))
        if step < ring - ring // 2:
            behind = lax.ppermute(behind, axis, backward)
            pieces.append((behind, (ring_pos + step) % ring))
    return pieces, ring


def ring_gather(block, axis):
    pieces, ring = ring_pieces(block, axis)
    gathered = jnp.zeros((ring,) + pieces[0][0].shape, block.dtype)
    for piece, source in pieces:
        gathered = lax.dynamic_update_index_in_dim(gathered, piece, source, 0)
    gathered = jnp.swapaxes(gathered, 0, 1)
    return gathered.reshape((2 * ring * block.shape[0],) + block.shape[1:])


def halving_scatter(partial, axis, order):
    size = lax.axis_size(axis)
    position = lax.axis_index(axis)
    state = partial
    for bit in order:
        half = state.shape[1] // 2
        mine = (position >> bit) & 1
        keep = lax.dynamic_slice_in_dim(state, mine * half, half, 1)
        send = lax.dynamic_slice_in_dim(state, (1 - mine) * half, half, 1)
        got = lax.ppermute(
            send.astype(jnp.bfloat16), axis, [(i, i ^ (1 << bit)) for i in range(size)]
        )
        state = keep + got.astype(jnp.float32)
    return state


def attend_piece(state_now, kv_piece, key_frame, queries, query_frame, query_first, head_dim):
    run_max, run_sum, accumulated = state_now
    key_part = kv_piece[:, :, :head_dim]
    value_part = kv_piece[:, :, head_dim:]
    scores = jnp.einsum(
        "nhe,mhe->nhm", queries, key_part, preferred_element_type=jnp.float32
    ) * head_dim ** (-0.5)
    allowed = (key_frame[None, :] <= query_frame[:, None]) & (
        key_frame[None, :] >= query_first[:, None]
    )
    masked = jnp.where(allowed[:, None, :], scores, NEG)
    new_max = jnp.maximum(run_max, masked.max(-1))
    exponent = jnp.where(allowed[:, None, :], jnp.exp(masked - new_max[..., None]), 0.0)
    factor = jnp.exp(run_max - new_max)
    run_sum = run_sum * factor + exponent.sum(-1)
    accumulated = accumulated * factor[..., None] + jnp.einsum(
        "nhm,mhe->nhe",
        exponent.astype(jnp.bfloat16),
        value_part,
        preferred_element_type=jnp.float32,
    )
    return (new_max, run_sum, accumulated)


def per_device(
    latents, timestep, offsets, qkv_weight, mod_weight, gate_weight, out_weight, conv_weight
):
    tok_rows = latents.shape[0]
    heads_here = qkv_weight.shape[1]
    head_dim = out_weight.shape[2]
    chan_here = gate_weight.shape[1]
    frame_size = HH * WW
    frames_here = tok_rows // frame_size
    position = lax.axis_index("ctx")
    column = lax.axis_index("fsdp")
    time_act = time_features(timestep, gate_weight.shape[0])
    gate_vec = jnp.dot(time_act, gate_weight, preferred_element_type=jnp.float32)
    float_rows = latents.astype(jnp.float32)
    centred = float_rows - float_rows.mean(-1, keepdims=True)
    variance = (centred * centred).mean(-1, keepdims=True)
    normed = centred * lax.rsqrt(variance + EPS)

    rows_here = qkv_weight.shape[0]
    qkv_width = qkv_weight.shape[2]
    qkv_cols = heads_here * qkv_width
    out_cols = heads_here * head_dim
    width = qkv_cols + out_cols
    local_shares = jnp.einsum(
        "rjt,t->rj", mod_weight, time_act, preferred_element_type=jnp.float32
    )
    shares_hi = local_shares.astype(jnp.bfloat16)
    shares_lo = (local_shares - shares_hi.astype(jnp.float32)).astype(jnp.bfloat16)
    share_count = 4 * rows_here
    extra_rows = 8 * ((share_count + 8 * width - 1) // (8 * width))
    share_block = jnp.zeros((extra_rows * width,), jnp.bfloat16)
    share_block = share_block.at[:share_count].set(
        jnp.concatenate([shares_hi, shares_lo], axis=1).reshape(share_count)
    )
    bundle = jnp.concatenate(
        [
            jnp.concatenate(
                [
                    qkv_weight.reshape(rows_here, qkv_cols),
                    out_weight.reshape(rows_here, out_cols),
                ],
                axis=1,
            ),
            share_block.reshape(extra_rows, width),
        ],
        axis=0,
    )
    gathered = ring_gather(bundle, "ctx")
    blocks = gathered.shape[0] // bundle.shape[0]
    gathered = gathered.reshape(blocks, rows_here + extra_rows, width)
    full_rows = blocks * rows_here
    w_piece = gathered[:, :rows_here, :qkv_cols].reshape(full_rows, heads_here, qkv_width)
    o_piece = gathered[:, :rows_here, qkv_cols:].reshape(full_rows, heads_here, head_dim)
    share_bits = (
        gathered[:, rows_here:, :]
        .reshape(blocks, extra_rows * width)[:, :share_count]
        .reshape(full_rows, 4)
        .astype(jnp.float32)
    )
    shares = share_bits[:, :2] + share_bits[:, 2:]

    modulated = (normed * (1.0 + shares[:, 1]) + shares[:, 0]).astype(jnp.bfloat16)
    projected_qkv = jnp.einsum(
        "nr,rhc->nhc", modulated, w_piece, preferred_element_type=jnp.float32
    ).astype(jnp.bfloat16)
    queries = projected_qkv[:, :, :head_dim]
    packed = projected_qkv[:, :, head_dim:]
    query_frame = position * frames_here + jnp.arange(tok_rows, dtype=jnp.int32) // frame_size
    local_first = lax.dynamic_slice_in_dim(offsets, position * frames_here, frames_here, 0)
    query_first = jnp.repeat(local_first, frame_size)
    state = (
        jnp.full((tok_rows, heads_here), NEG, jnp.float32),
        jnp.zeros((tok_rows, heads_here), jnp.float32),
        jnp.zeros((tok_rows, heads_here, head_dim), jnp.float32),
    )
    kv_pieces, ring = ring_pieces(packed, "ctx")
    token_ids = jnp.arange(tok_rows, dtype=jnp.int32)
    for piece, source in kv_pieces:
        key_frame = (
            jnp.concatenate(
                [source * tok_rows + token_ids, (ring + source) * tok_rows + token_ids]
            )
            // frame_size
        )
        state = attend_piece(
            state,
            piece.reshape((2 * tok_rows,) + piece.shape[2:]),
            key_frame,
            queries,
            query_frame,
            query_first,
            head_dim,
        )
    run_max, run_sum, accumulated = state_now
    key_part = kv_piece[:, :, :head_dim]
    value_part = kv_piece[:, :, head_dim:]
    scores = jnp.einsum(
        "nhe,mhe->nhm", queries, key_part, preferred_element_type=jnp.float32
    ) * head_dim ** (-0.5)
    allowed = (key_frame[None, :] <= query_frame[:, None]) & (
        key_frame[None, :] >= query_first[:, None]
    )
    masked = jnp.where(allowed[:, None, :], scores, NEG)
    new_max = jnp.maximum(run_max, masked.max(-1))
    exponent = jnp.where(allowed[:, None, :], jnp.exp(masked - new_max[..., None]), 0.0)
    factor = jnp.exp(run_max - new_max)
    run_sum = run_sum * factor + exponent.sum(-1)
    accumulated = accumulated * factor[..., None] + jnp.einsum(
        "nhm,mhe->nhe",
        exponent.astype(jnp.bfloat16),
        value_part,
        preferred_element_type=jnp.float32,
    )
    return (new_max, run_sum, accumulated)


def per_device(
    latents, timestep, offsets, qkv_weight, mod_weight, gate_weight, out_weight, conv_weight
):
    tok_rows = latents.shape[0]
    heads_here = qkv_weight.shape[1]
    head_dim = out_weight.shape[2]
    chan_here = gate_weight.shape[1]
    frame_size = HH * WW
    frames_here = tok_rows // frame_size
    position = lax.axis_index("ctx")
    column = lax.axis_index("fsdp")
    time_act = time_features(timestep, gate_weight.shape[0])
    gate_vec = jnp.dot(time_act, gate_weight, preferred_element_type=jnp.float32)
    float_rows = latents.astype(jnp.float32)
    centred = float_rows - float_rows.mean(-1, keepdims=True)
    variance = (centred * centred).mean(-1, keepdims=True)
    normed = centred * lax.rsqrt(variance + EPS)

    rows_here = qkv_weight.shape[0]
    qkv_width = qkv_weight.shape[2]
    qkv_cols = heads_here * qkv_width
    out_cols = heads_here * head_dim
    width = qkv_cols + out_cols
    local_shares = jnp.einsum(
        "rjt,t->rj", mod_weight, time_act, preferred_element_type=jnp.float32
    )
    shares_hi = local_shares.astype(jnp.bfloat16)
    shares_lo = (local_shares - shares_hi.astype(jnp.float32)).astype(jnp.bfloat16)
    share_count = 4 * rows_here
    extra_rows = 8 * ((share_count + 8 * width - 1) // (8 * width))
    share_block = jnp.zeros((extra_rows * width,), jnp.bfloat16)
    share_block = share_block.at[:share_count].set(
        jnp.concatenate([shares_hi, shares_lo], axis=1).reshape(share_count)
    )
    bundle = jnp.concatenate(
        [
            jnp.concatenate(
                [
                    qkv_weight.reshape(rows_here, qkv_cols),
                    out_weight.reshape(rows_here, out_cols),
                ],
                axis=1,
            ),
            share_block.reshape(extra_rows, width),
        ],
        axis=0,
    )
    gathered = ring_gather(bundle, "ctx")
    blocks = gathered.shape[0] // bundle.shape[0]
    gathered = gathered.reshape(blocks, rows_here + extra_rows, width)
    full_rows = blocks * rows_here
    w_piece = gathered[:, :rows_here, :qkv_cols].reshape(full_rows, heads_here, qkv_width)
    o_piece = gathered[:, :rows_here, qkv_cols:].reshape(full_rows, heads_here, head_dim)
    share_bits = (
        gathered[:, rows_here:, :]
        .reshape(blocks, extra_rows * width)[:, :share_count]
        .reshape(full_rows, 4)
        .astype(jnp.float32)
    )
    shares = share_bits[:, :2] + share_bits[:, 2:]

    modulated = (normed * (1.0 + shares[:, 1]) + shares[:, 0]).astype(jnp.bfloat16)
    projected_qkv = jnp.einsum(
        "nr,rhc->nhc", modulated, w_piece, preferred_element_type=jnp.float32
    ).astype(jnp.bfloat16)
    queries = projected_qkv[:, :, :head_dim]
    packed = projected_qkv[:, :, head_dim:]
    query_frame = position * frames_here + jnp.arange(tok_rows, dtype=jnp.int32) // frame_size
    local_first = lax.dynamic_slice_in_dim(offsets, position * frames_here, frames_here, 0)
    query_first = jnp.repeat(local_first, frame_size)
    state = (
        jnp.full((tok_rows, heads_here), NEG, jnp.float32),
        jnp.zeros((tok_rows, heads_here), jnp.float32),
        jnp.zeros((tok_rows, heads_here, head_dim), jnp.float32),
    )
    kv_pieces, ring = ring_pieces(packed, "ctx")
    token_ids = jnp.arange(tok_rows, dtype=jnp.int32)
    step_groups = [kv_pieces[:1]] + [
        kv_pieces[i : i + 2] for i in range(1, len(kv_pieces), 2)
    ]
    for group in step_groups:
        key_frame = (
            jnp.concatenate(
                [
                    jnp.concatenate(
                        [source * tok_rows + token_ids, (ring + source) * tok_rows + token_ids]
                    )
                    for _, source in group
                ]
            )
            // frame_size
        )
        keys_values = jnp.concatenate(
            [piece.reshape((2 * tok_rows,) + piece.shape[2:]) for piece, _ in group]
        )
        state = attend_piece(
            state, keys_values, key_frame, queries, query_frame, query_first, head_dim
        )
    run_max, run_sum, accumulated = state
    attended = (accumulated / run_sum[..., None]).astype(jnp.bfloat16)
    size = lax.axis_size("fsdp")
    bits = size.bit_length() - 1
    middle = list(range(1, bits - 1))
    half_rows = tok_rows // 2
    orders = [[0, bits - 1] + middle, [0] + middle + [bits - 1]]
    head_parts = []
    for part, order in enumerate(orders):
        by_bit = o_piece.reshape((2,) * bits + (full_rows // size,) + o_piece.shape[1:])
        permuted = jnp.transpose(
            by_bit,
            [bits - 1 - bit for bit in order] + list(range(bits, by_bit.ndim)),
        )
        partial_out = jnp.einsum(
            "nhe,rhe->nr",
            attended[part * half_rows : (part + 1) * half_rows],
            permuted.reshape(o_piece.shape),
            preferred_element_type=jnp.float32,
        )
        head_parts.append(halving_scatter(partial_out, "fsdp", order))
    head_total = jnp.concatenate(head_parts, axis=0)
    own_chan = lax.dynamic_slice_in_dim(latents, column * chan_here, chan_here, 1)
    before = passed_along(own_chan, "ctx", 1)
    stacked = (
        jnp.concatenate([before, own_chan], 0)
        .astype(jnp.float32)
        .reshape(frames_here + 2, HH, WW, chan_here)
    )
    padded = jnp.pad(stacked, ((0, 0), (1, 1), (1, 1), (0, 0)))
    convolved = jnp.zeros((frames_here, HH, WW, chan_here), jnp.float32)
    for time_lag in range(3):
        for row_shift in range(3):
            for col_shift in range(3):
                tap = conv_weight[time_lag, row_shift, col_shift].astype(jnp.float32)
                convolved = (
                    convolved
                    + tap
                    * padded[
                        2 - time_lag : 2 - time_lag + frames_here,
                        row_shift : row_shift + HH,
                        col_shift : col_shift + WW,
                    ]
                )
    residual = own_chan.astype(jnp.float32)
    mixed = residual + gate_vec * head_total + convolved.reshape(tok_rows, chan_here)
    return mixed.astype(jnp.bfloat16)


def solution(mesh):
    in_specs = (
        P("ctx", None),
        P(),
        P(),
        P("ctx", "fsdp", None),
        P("ctx", None, None),
        P(None, "fsdp"),
        P("ctx", "fsdp", None),
        P(None, None, None, "fsdp"),
    )
    out_specs = P("ctx", "fsdp")
    return jax.shard_map(
        per_device, mesh=mesh, in_specs=in_specs, out_specs=out_specs, check_vma=False
    )
```

```python
import math

import jax
import jax.numpy as jnp
from jax import lax
from jax.sharding import PartitionSpec as P

HH = 10
WW = 16


EPS = 1e-06
NEG = -1e30


def passed_along(block, axis, distance):
    devices = range(lax.axis_size(axis))
    route = [(i - distance, i) for i in devices if i - distance in devices]
    return lax.ppermute(block, axis, route)


def time_features(timestep, embed_width):
    half_width = embed_width // 2
    freqs = jnp.exp(-math.log(10000.0) * jnp.arange(half_width, dtype=jnp.float32) / half_width)
    angles = timestep[0].astype(jnp.float32) * freqs
    embed = jnp.concatenate([jnp.cos(angles), jnp.sin(angles)])
    return jax.nn.silu(embed).astype(jnp.bfloat16)


def ring_pieces(block, axis):
    size = lax.axis_size(axis)
    ring = size // 2
    position = lax.axis_index(axis)
    partner = lax.ppermute(block, axis, [(i, (i + ring) % size) for i in range(size)])
    pair = jnp.where(
        position // ring == 0, jnp.stack([block, partner]), jnp.stack([partner, block])
    )
    ring_pos = position % ring
    forward = [(y * ring + a, y * ring + (a + 1) % ring) for y in range(2) for a in range(ring)]
    backward = [(y * ring + a, y * ring + (a - 1) % ring) for y in range(2) for a in range(ring)]
    pieces = [(pair, ring_pos)]
    ahead = pair
    behind = pair
    for step in range(1, ring // 2 + 1):
        ahead = lax.ppermute(ahead, axis, forward)
        pieces.append((ahead, (ring_pos - step) % ring))
        if step < ring - ring // 2:
            behind = lax.ppermute(behind, axis, backward)
            pieces.append((behind, (ring_pos + step) % ring))
    return pieces, ring


def ring_gather(block, axis):
    pieces, ring = ring_pieces(block, axis)
    gathered = jnp.zeros((ring,) + pieces[0][0].shape, block.dtype)
    for piece, source in pieces:
        gathered = lax.dynamic_update_index_in_dim(gathered, piece, source, 0)
    gathered = jnp.swapaxes(gathered, 0, 1)
    return gathered.reshape((2 * ring * block.shape[0],) + block.shape[1:])


def halving_scatter(partial, axis, order):
    size = lax.axis_size(axis)
    position = lax.axis_index(axis)
    state = partial
    for bit in order:
        half = state.shape[1] // 2
        mine = (position >> bit) & 1
        keep = lax.dynamic_slice_in_dim(state, mine * half, half, 1)
        send = lax.dynamic_slice_in_dim(state, (1 - mine) * half, half, 1)
        got = lax.ppermute(
            send.astype(jnp.bfloat16), axis, [(i, i ^ (1 << bit)) for i in range(size)]
        )
        state = keep + got.astype(jnp.float32)
    return state


def attend_piece(state_now, kv_piece, key_frame, queries, query_frame, query_first, head_dim):
    run_max, run_sum, accumulated = state_now
    key_part = kv_piece[:, :, :head_dim]
    value_part = kv_piece[:, :, head_dim:]
    scores = jnp.einsum(
        "nhe,mhe->nhm", queries, key_part, preferred_element_type=jnp.float32
    ) * head_dim ** (-0.5)
    allowed = (key_frame[None, :] <= query_frame[:, None]) & (
        key_frame[None, :] >= query_first[:, None]
    )
    masked = jnp.where(allowed[:, None, :], scores, NEG)
    new_max = jnp.maximum(run_max, masked.max(-1))
    exponent = jnp.where(allowed[:, None, :], jnp.exp(masked - new_max[..., None]), 0.0)
    factor = jnp.exp(run_max - new_max)
    run_sum = run_sum * factor + exponent.sum(-1)
    accumulated = accumulated * factor[..., None] + jnp.einsum(
        "nhm,mhe->nhe",
        exponent.astype(jnp.bfloat16),
        value_part,
        preferred_element_type=jnp.float32,
    )
    return (new_max, run_sum, accumulated)


def per_device(
    latents, timestep, offsets, qkv_weight, mod_weight, gate_weight, out_weight, conv_weight
):
    tok_rows = latents.shape[0]
    heads_here = qkv_weight.shape[1]
    head_dim = out_weight.shape[2]
    chan_here = gate_weight.shape[1]
    frame_size = HH * WW
    frames_here = tok_rows // frame_size
    position = lax.axis_index("ctx")
    column = lax.axis_index("fsdp")
    time_act = time_features(timestep, gate_weight.shape[0])
    gate_vec = jnp.dot(time_act, gate_weight, preferred_element_type=jnp.float32)
    float_rows = latents.astype(jnp.float32)
    centred = float_rows - float_rows.mean(-1, keepdims=True)
    variance = (centred * centred).mean(-1, keepdims=True)
    normed = centred * lax.rsqrt(variance + EPS)

    rows_here = qkv_weight.shape[0]
    qkv_width = qkv_weight.shape[2]
    qkv_cols = heads_here * qkv_width
    out_cols = heads_here * head_dim
    width = qkv_cols + out_cols
    local_shares = jnp.einsum(
        "rjt,t->rj", mod_weight, time_act, preferred_element_type=jnp.float32
    )
    shares_hi = local_shares.astype(jnp.bfloat16)
    shares_lo = (local_shares - shares_hi.astype(jnp.float32)).astype(jnp.bfloat16)
    share_count = 4 * rows_here
    extra_rows = 8 * ((share_count + 8 * width - 1) // (8 * width))
    share_block = jnp.zeros((extra_rows * width,), jnp.bfloat16)
    share_block = share_block.at[:share_count].set(
        jnp.concatenate([shares_hi, shares_lo], axis=1).reshape(share_count)
    )
    bundle = jnp.concatenate(
        [
            jnp.concatenate(
                [
                    qkv_weight.reshape(rows_here, qkv_cols),
                    out_weight.reshape(rows_here, out_cols),
                ],
                axis=1,
            ),
            share_block.reshape(extra_rows, width),
        ],
        axis=0,
    )
    gathered = ring_gather(bundle, "ctx")
    blocks = gathered.shape[0] // bundle.shape[0]
    gathered = gathered.reshape(blocks, rows_here + extra_rows, width)
    full_rows = blocks * rows_here
    w_piece = gathered[:, :rows_here, :qkv_cols].reshape(full_rows, heads_here, qkv_width)
    o_piece = gathered[:, :rows_here, qkv_cols:].reshape(full_rows, heads_here, head_dim)
    share_bits = (
        gathered[:, rows_here:, :]
        .reshape(blocks, extra_rows * width)[:, :share_count]
        .reshape(full_rows, 4)
        .astype(jnp.float32)
    )
    shares = share_bits[:, :2] + share_bits[:, 2:]

    modulated = (normed * (1.0 + shares[:, 1]) + shares[:, 0]).astype(jnp.bfloat16)
    projected_qkv = jnp.einsum(
        "nr,rhc->nhc", modulated, w_piece, preferred_element_type=jnp.float32
    ).astype(jnp.bfloat16)
    queries = projected_qkv[:, :, :head_dim]
    packed = projected_qkv[:, :, head_dim:]
    query_frame = position * frames_here + jnp.arange(tok_rows, dtype=jnp.int32) // frame_size
    local_first = lax.dynamic_slice_in_dim(offsets, position * frames_here, frames_here, 0)
    query_first = jnp.repeat(local_first, frame_size)
    state = (
        jnp.full((tok_rows, heads_here), NEG, jnp.float32),
        jnp.zeros((tok_rows, heads_here), jnp.float32),
        jnp.zeros((tok_rows, heads_here, head_dim), jnp.float32),
    )
    size = lax.axis_size("ctx")
    ring = size // 2
    partner = lax.ppermute(packed, "ctx", [(i, (i + ring) % size) for i in range(size)])
    pair = jnp.where(
        position // ring == 0, jnp.stack([packed, partner]), jnp.stack([partner, packed])
    )
    ring_pos = position % ring
    forward = [(y * ring + a, y * ring + (a + 1) % ring) for y in range(2) for a in range(ring)]
    backward = [(y * ring + a, y * ring + (a - 1) % ring) for y in range(2) for a in range(ring)]
    token_ids = jnp.arange(tok_rows, dtype=jnp.int32)

    def fold(state_in, piece, source):
        key_frame = (
            jnp.concatenate(
                [source * tok_rows + token_ids, (ring + source) * tok_rows + token_ids]
            )
            // frame_size
        )
        return attend_piece(
            state_in,
            piece.reshape((2 * tok_rows,) + piece.shape[2:]),
            key_frame,
            queries,
            query_frame,
            query_first,
            head_dim,
        )

    states = [fold(state, pair, ring_pos)]
    ahead = pair
    behind = pair
    for step in range(1, ring // 2 + 1):
        if step > 1:
            ahead, behind, _ = lax.optimization_barrier((ahead, behind, states[step - 2]))
        ahead = lax.ppermute(ahead, "ctx", forward)
        has_behind = step < ring - ring // 2
        if has_behind:
            behind = lax.ppermute(behind, "ctx", backward)
        folded = fold(states[-1], ahead, (ring_pos - step) % ring)
        if has_behind:
            folded = fold(folded, behind, (ring_pos + step) % ring)
        states.append(folded)
    state = states[-1]
    run_max, run_sum, accumulated = state_now
    key_part = kv_piece[:, :, :head_dim]
    value_part = kv_piece[:, :, head_dim:]
    scores = jnp.einsum(
        "nhe,mhe->nhm", queries, key_part, preferred_element_type=jnp.float32
    ) * head_dim ** (-0.5)
    allowed = (key_frame[None, :] <= query_frame[:, None]) & (
        key_frame[None, :] >= query_first[:, None]
    )
    masked = jnp.where(allowed[:, None, :], scores, NEG)
    new_max = jnp.maximum(run_max, masked.max(-1))
    exponent = jnp.where(allowed[:, None, :], jnp.exp(masked - new_max[..., None]), 0.0)
    factor = jnp.exp(run_max - new_max)
    run_sum = run_sum * factor + exponent.sum(-1)
    accumulated = accumulated * factor[..., None] + jnp.einsum(
        "nhm,mhe->nhe",
        exponent.astype(jnp.bfloat16),
        value_part,
        preferred_element_type=jnp.float32,
    )
    return (new_max, run_sum, accumulated)


def per_device(
    latents, timestep, offsets, qkv_weight, mod_weight, gate_weight, out_weight, conv_weight
):
    tok_rows = latents.shape[0]
    heads_here = qkv_weight.shape[1]
    head_dim = out_weight.shape[2]
    chan_here = gate_weight.shape[1]
    frame_size = HH * WW
    frames_here = tok_rows // frame_size
    position = lax.axis_index("ctx")
    column = lax.axis_index("fsdp")
    time_act = time_features(timestep, gate_weight.shape[0])
    gate_vec = jnp.dot(time_act, gate_weight, preferred_element_type=jnp.float32)
    float_rows = latents.astype(jnp.float32)
    centred = float_rows - float_rows.mean(-1, keepdims=True)
    variance = (centred * centred).mean(-1, keepdims=True)
    normed = centred * lax.rsqrt(variance + EPS)

    rows_here = qkv_weight.shape[0]
    qkv_width = qkv_weight.shape[2]
    qkv_cols = heads_here * qkv_width
    out_cols = heads_here * head_dim
    width = qkv_cols + out_cols
    local_shares = jnp.einsum(
        "rjt,t->rj", mod_weight, time_act, preferred_element_type=jnp.float32
    )
    shares_hi = local_shares.astype(jnp.bfloat16)
    shares_lo = (local_shares - shares_hi.astype(jnp.float32)).astype(jnp.bfloat16)
    share_count = 4 * rows_here
    extra_rows = 8 * ((share_count + 8 * width - 1) // (8 * width))
    share_block = jnp.zeros((extra_rows * width,), jnp.bfloat16)
    share_block = share_block.at[:share_count].set(
        jnp.concatenate([shares_hi, shares_lo], axis=1).reshape(share_count)
    )
    bundle = jnp.concatenate(
        [
            jnp.concatenate(
                [
                    qkv_weight.reshape(rows_here, qkv_cols),
                    out_weight.reshape(rows_here, out_cols),
                ],
                axis=1,
            ),
            share_block.reshape(extra_rows, width),
        ],
        axis=0,
    )
    gathered = ring_gather(bundle, "ctx")
    blocks = gathered.shape[0] // bundle.shape[0]
    gathered = gathered.reshape(blocks, rows_here + extra_rows, width)
    full_rows = blocks * rows_here
    w_piece = gathered[:, :rows_here, :qkv_cols].reshape(full_rows, heads_here, qkv_width)
    o_piece = gathered[:, :rows_here, qkv_cols:].reshape(full_rows, heads_here, head_dim)
    share_bits = (
        gathered[:, rows_here:, :]
        .reshape(blocks, extra_rows * width)[:, :share_count]
        .reshape(full_rows, 4)
        .astype(jnp.float32)
    )
    shares = share_bits[:, :2] + share_bits[:, 2:]

    modulated = (normed * (1.0 + shares[:, 1]) + shares[:, 0]).astype(jnp.bfloat16)
    projected_qkv = jnp.einsum(
        "nr,rhc->nhc", modulated, w_piece, preferred_element_type=jnp.float32
    ).astype(jnp.bfloat16)
    queries = projected_qkv[:, :, :head_dim]
    packed = projected_qkv[:, :, head_dim:]
    query_frame = position * frames_here + jnp.arange(tok_rows, dtype=jnp.int32) // frame_size
    local_first = lax.dynamic_slice_in_dim(offsets, position * frames_here, frames_here, 0)
    query_first = jnp.repeat(local_first, frame_size)
    state = (
        jnp.full((tok_rows, heads_here), NEG, jnp.float32),
        jnp.zeros((tok_rows, heads_here), jnp.float32),
        jnp.zeros((tok_rows, heads_here, head_dim), jnp.float32),
    )
    size = lax.axis_size("ctx")
    ring = size // 2
    partner = lax.ppermute(packed, "ctx", [(i, (i + ring) % size) for i in range(size)])
    pair = jnp.where(
        position // ring == 0, jnp.stack([packed, partner]), jnp.stack([partner, packed])
    )
    ring_pos = position % ring
    forward = [(y * ring + a, y * ring + (a + 1) % ring) for y in range(2) for a in range(ring)]
    backward = [(y * ring + a, y * ring + (a - 1) % ring) for y in range(2) for a in range(ring)]
    token_ids = jnp.arange(tok_rows, dtype=jnp.int32)

    def fold(state_in, piece, source):
        key_frame = (
            jnp.concatenate(
                [source * tok_rows + token_ids, (ring + source) * tok_rows + token_ids]
            )
            // frame_size
        )
        return attend_piece(
            state_in,
            piece.reshape((2 * tok_rows,) + piece.shape[2:]),
            key_frame,
            queries,
            query_frame,
            query_first,
            head_dim,
        )

    ahead = pair
    behind = pair
    lagging = state
    state = fold(state, pair, ring_pos)
    for step in range(1, ring // 2 + 1):
        if step > 1:
            ahead, behind, lagging = lax.optimization_barrier((ahead, behind, lagging))
            state = lagging if step == 2 else state
        ahead = lax.ppermute(ahead, "ctx", forward)
        has_behind = step < ring - ring // 2
        if has_behind:
            behind = lax.ppermute(behind, "ctx", backward)
        lagging = state
        state = fold(state, ahead, (ring_pos - step) % ring)
        if has_behind:
            state = fold(state, behind, (ring_pos + step) % ring)
    run_max, run_sum, accumulated = state_now
    key_part = kv_piece[:, :, :head_dim]
    value_part = kv_piece[:, :, head_dim:]
    scores = jnp.einsum(
        "nhe,mhe->nhm", queries, key_part, preferred_element_type=jnp.float32
    ) * head_dim ** (-0.5)
    allowed = (key_frame[None, :] <= query_frame[:, None]) & (
        key_frame[None, :] >= query_first[:, None]
    )
    masked = jnp.where(allowed[:, None, :], scores, NEG)
    new_max = jnp.maximum(run_max, masked.max(-1))
    exponent = jnp.where(allowed[:, None, :], jnp.exp(masked - new_max[..., None]), 0.0)
    factor = jnp.exp(run_max - new_max)
    run_sum = run_sum * factor + exponent.sum(-1)
    accumulated = accumulated * factor[..., None] + jnp.einsum(
        "nhm,mhe->nhe",
        exponent.astype(jnp.bfloat16),
        value_part,
        preferred_element_type=jnp.float32,
    )
    return (new_max, run_sum, accumulated)


def per_device(
    latents, timestep, offsets, qkv_weight, mod_weight, gate_weight, out_weight, conv_weight
):
    tok_rows = latents.shape[0]
    heads_here = qkv_weight.shape[1]
    head_dim = out_weight.shape[2]
    chan_here = gate_weight.shape[1]
    frame_size = HH * WW
    frames_here = tok_rows // frame_size
    position = lax.axis_index("ctx")
    column = lax.axis_index("fsdp")
    time_act = time_features(timestep, gate_weight.shape[0])
    gate_vec = jnp.dot(time_act, gate_weight, preferred_element_type=jnp.float32)
    float_rows = latents.astype(jnp.float32)
    centred = float_rows - float_rows.mean(-1, keepdims=True)
    variance = (centred * centred).mean(-1, keepdims=True)
    normed = centred * lax.rsqrt(variance + EPS)

    rows_here = qkv_weight.shape[0]
    qkv_width = qkv_weight.shape[2]
    qkv_cols = heads_here * qkv_width
    out_cols = heads_here * head_dim
    width = qkv_cols + out_cols
    local_shares = jnp.einsum(
        "rjt,t->rj", mod_weight, time_act, preferred_element_type=jnp.float32
    )
    shares_hi = local_shares.astype(jnp.bfloat16)
    shares_lo = (local_shares - shares_hi.astype(jnp.float32)).astype(jnp.bfloat16)
    share_count = 4 * rows_here
    extra_rows = 8 * ((share_count + 8 * width - 1) // (8 * width))
    share_block = jnp.zeros((extra_rows * width,), jnp.bfloat16)
    share_block = share_block.at[:share_count].set(
        jnp.concatenate([shares_hi, shares_lo], axis=1).reshape(share_count)
    )
    bundle = jnp.concatenate(
        [
            jnp.concatenate(
                [
                    qkv_weight.reshape(rows_here, qkv_cols),
                    out_weight.reshape(rows_here, out_cols),
                ],
                axis=1,
            ),
            share_block.reshape(extra_rows, width),
        ],
        axis=0,
    )
    gathered = ring_gather(bundle, "ctx")
    blocks = gathered.shape[0] // bundle.shape[0]
    gathered = gathered.reshape(blocks, rows_here + extra_rows, width)
    full_rows = blocks * rows_here
    w_piece = gathered[:, :rows_here, :qkv_cols].reshape(full_rows, heads_here, qkv_width)
    o_piece = gathered[:, :rows_here, qkv_cols:].reshape(full_rows, heads_here, head_dim)
    share_bits = (
        gathered[:, rows_here:, :]
        .reshape(blocks, extra_rows * width)[:, :share_count]
        .reshape(full_rows, 4)
        .astype(jnp.float32)
    )
    shares = share_bits[:, :2] + share_bits[:, 2:]

    modulated = (normed * (1.0 + shares[:, 1]) + shares[:, 0]).astype(jnp.bfloat16)
    projected_qkv = jnp.einsum(
        "nr,rhc->nhc", modulated, w_piece, preferred_element_type=jnp.float32
    ).astype(jnp.bfloat16)
    queries = projected_qkv[:, :, :head_dim]
    packed = projected_qkv[:, :, head_dim:]
    query_frame = position * frames_here + jnp.arange(tok_rows, dtype=jnp.int32) // frame_size
    local_first = lax.dynamic_slice_in_dim(offsets, position * frames_here, frames_here, 0)
    query_first = jnp.repeat(local_first, frame_size)
    state = (
        jnp.full((tok_rows, heads_here), NEG, jnp.float32),
        jnp.zeros((tok_rows, heads_here), jnp.float32),
        jnp.zeros((tok_rows, heads_here, head_dim), jnp.float32),
    )
    kv_pieces, ring = ring_pieces(packed, "ctx")
    token_ids = jnp.arange(tok_rows, dtype=jnp.int32)
    for piece, source in kv_pieces:
        key_frame = (
            jnp.concatenate(
                [source * tok_rows + token_ids, (ring + source) * tok_rows + token_ids]
            )
            // frame_size
        )
        state = attend_piece(
            state,
            piece.reshape((2 * tok_rows,) + piece.shape[2:]),
            key_frame,
            queries,
            query_frame,
            query_first,
            head_dim,
        )
    run_max, run_sum, accumulated = state_now
    key_part = kv_piece[:, :, :head_dim]
    value_part = kv_piece[:, :, head_dim:]
    scores = jnp.einsum(
        "nhe,mhe->nhm", queries, key_part, preferred_element_type=jnp.float32
    ) * head_dim ** (-0.5)
    allowed = (key_frame[None, :] <= query_frame[:, None]) & (
        key_frame[None, :] >= query_first[:, None]
    )
    masked = jnp.where(allowed[:, None, :], scores, NEG)
    new_max = jnp.maximum(run_max, masked.max(-1))
    exponent = jnp.where(allowed[:, None, :], jnp.exp(masked - new_max[..., None]), 0.0)
    factor = jnp.exp(run_max - new_max)
    run_sum = run_sum * factor + exponent.sum(-1)
    accumulated = accumulated * factor[..., None] + jnp.einsum(
        "nhm,mhe->nhe",
        exponent.astype(jnp.bfloat16),
        value_part,
        preferred_element_type=jnp.float32,
    )
    return (new_max, run_sum, accumulated)


def per_device(
    latents, timestep, offsets, qkv_weight, mod_weight, gate_weight, out_weight, conv_weight
):
    tok_rows = latents.shape[0]
    heads_here = qkv_weight.shape[1]
    head_dim = out_weight.shape[2]
    chan_here = gate_weight.shape[1]
    frame_size = HH * WW
    frames_here = tok_rows // frame_size
    position = lax.axis_index("ctx")
    column = lax.axis_index("fsdp")
    time_act = time_features(timestep, gate_weight.shape[0])
    gate_vec = jnp.dot(time_act, gate_weight, preferred_element_type=jnp.float32)
    float_rows = latents.astype(jnp.float32)
    centred = float_rows - float_rows.mean(-1, keepdims=True)
    variance = (centred * centred).mean(-1, keepdims=True)
    normed = centred * lax.rsqrt(variance + EPS)

    rows_here = qkv_weight.shape[0]
    qkv_width = qkv_weight.shape[2]
    qkv_cols = heads_here * qkv_width
    out_cols = heads_here * head_dim
    width = qkv_cols + out_cols
    local_shares = jnp.einsum(
        "rjt,t->rj", mod_weight, time_act, preferred_element_type=jnp.float32
    )
    shares_hi = local_shares.astype(jnp.bfloat16)
    shares_lo = (local_shares - shares_hi.astype(jnp.float32)).astype(jnp.bfloat16)
    share_count = 4 * rows_here
    extra_rows = 8 * ((share_count + 8 * width - 1) // (8 * width))
    share_block = jnp.zeros((extra_rows * width,), jnp.bfloat16)
    share_block = share_block.at[:share_count].set(
        jnp.concatenate([shares_hi, shares_lo], axis=1).reshape(share_count)
    )
    bundle = jnp.concatenate(
        [
            jnp.concatenate(
                [
                    qkv_weight.reshape(rows_here, qkv_cols),
                    out_weight.reshape(rows_here, out_cols),
                ],
                axis=1,
            ),
            share_block.reshape(extra_rows, width),
        ],
        axis=0,
    )
    gathered = ring_gather(bundle, "ctx")
    blocks = gathered.shape[0] // bundle.shape[0]
    gathered = gathered.reshape(blocks, rows_here + extra_rows, width)
    full_rows = blocks * rows_here
    w_piece = gathered[:, :rows_here, :qkv_cols].reshape(full_rows, heads_here, qkv_width)
    o_piece = gathered[:, :rows_here, qkv_cols:].reshape(full_rows, heads_here, head_dim)
    share_bits = (
        gathered[:, rows_here:, :]
        .reshape(blocks, extra_rows * width)[:, :share_count]
        .reshape(full_rows, 4)
        .astype(jnp.float32)
    )
    shares = share_bits[:, :2] + share_bits[:, 2:]

    modulated = (normed * (1.0 + shares[:, 1]) + shares[:, 0]).astype(jnp.bfloat16)
    projected_qkv = jnp.einsum(
        "nr,rhc->nhc", modulated, w_piece, preferred_element_type=jnp.float32
    ).astype(jnp.bfloat16)
    queries = projected_qkv[:, :, :head_dim]
    packed = projected_qkv[:, :, head_dim:]
    query_frame = position * frames_here + jnp.arange(tok_rows, dtype=jnp.int32) // frame_size
    local_first = lax.dynamic_slice_in_dim(offsets, position * frames_here, frames_here, 0)
    query_first = jnp.repeat(local_first, frame_size)
    state = (
        jnp.full((tok_rows, heads_here), NEG, jnp.float32),
        jnp.zeros((tok_rows, heads_here), jnp.float32),
        jnp.zeros((tok_rows, heads_here, head_dim), jnp.float32),
    )
    kv_pieces, ring = ring_pieces(packed, "ctx")
    token_ids = jnp.arange(tok_rows, dtype=jnp.int32)
    step_groups = [kv_pieces[:1]] + [
        kv_pieces[i : i + 2] for i in range(1, len(kv_pieces), 2)
    ]
    for group in step_groups:
        key_frame = (
            jnp.concatenate(
                [
                    jnp.concatenate(
                        [source * tok_rows + token_ids, (ring + source) * tok_rows + token_ids]
                    )
                    for _, source in group
                ]
            )
            // frame_size
        )
        keys_values = jnp.concatenate(
            [piece.reshape((2 * tok_rows,) + piece.shape[2:]) for piece, _ in group]
        )
        state = attend_piece(
            state, keys_values, key_frame, queries, query_frame, query_first, head_dim
        )
    run_max, run_sum, accumulated = state
    attended = (accumulated / run_sum[..., None]).astype(jnp.bfloat16)
    size = lax.axis_size("fsdp")
    bits = size.bit_length() - 1
    middle = list(range(1, bits - 1))
    half_rows = tok_rows // 2
    orders = [[0, bits - 1] + middle, [0] + middle + [bits - 1]]
    head_parts = []
    for part, order in enumerate(orders):
        by_bit = o_piece.reshape((2,) * bits + (full_rows // size,) + o_piece.shape[1:])
        permuted = jnp.transpose(
            by_bit,
            [bits - 1 - bit for bit in order] + list(range(bits, by_bit.ndim)),
        )
        partial_out = jnp.einsum(
            "nhe,rhe->nr",
            attended[part * half_rows : (part + 1) * half_rows],
            permuted.reshape(o_piece.shape),
            preferred_element_type=jnp.float32,
        )
        head_parts.append(halving_scatter(partial_out, "fsdp", order))
    head_total = jnp.concatenate(head_parts, axis=0)
    own_chan = lax.dynamic_slice_in_dim(latents, column * chan_here, chan_here, 1)
    before = passed_along(own_chan, "ctx", 1)
    stacked = (
        jnp.concatenate([before, own_chan], 0)
        .astype(jnp.float32)
        .reshape(frames_here + 2, HH, WW, chan_here)
    )
    padded = jnp.pad(stacked, ((0, 0), (1, 1), (1, 1), (0, 0)))
    convolved = jnp.zeros((frames_here, HH, WW, chan_here), jnp.float32)
    for time_lag in range(3):
        for row_shift in range(3):
            for col_shift in range(3):
                tap = conv_weight[time_lag, row_shift, col_shift].astype(jnp.float32)
                convolved = (
                    convolved
                    + tap
                    * padded[
                        2 - time_lag : 2 - time_lag + frames_here,
                        row_shift : row_shift + HH,
                        col_shift : col_shift + WW,
                    ]
                )
    residual = own_chan.astype(jnp.float32)
    mixed = residual + gate_vec * head_total + convolved.reshape(tok_rows, chan_here)
    return mixed.astype(jnp.bfloat16)


def solution(mesh):
    in_specs = (
        P("ctx", None),
        P(),
        P(),
        P("ctx", "fsdp", None),
        P("ctx", None, None),
        P(None, "fsdp"),
        P("ctx", "fsdp", None),
        P(None, None, None, "fsdp"),
    )
    out_specs = P("ctx", "fsdp")
    return jax.shard_map(
        per_device, mesh=mesh, in_specs=in_specs, out_specs=out_specs, check_vma=False
    )
```

```python
import math

import jax
import jax.numpy as jnp
from jax import lax
from jax.sharding import PartitionSpec as P

HH = 10
WW = 16


EPS = 1e-06
NEG = -1e30


def passed_along(block, axis, distance):
    devices = range(lax.axis_size(axis))
    route = [(i - distance, i) for i in devices if i - distance in devices]
    return lax.ppermute(block, axis, route)


def time_features(timestep, embed_width):
    half_width = embed_width // 2
    freqs = jnp.exp(-math.log(10000.0) * jnp.arange(half_width, dtype=jnp.float32) / half_width)
    angles = timestep[0].astype(jnp.float32) * freqs
    embed = jnp.concatenate([jnp.cos(angles), jnp.sin(angles)])
    return jax.nn.silu(embed).astype(jnp.bfloat16)


def ring_pieces(block, axis):
    size = lax.axis_size(axis)
    ring = size // 2
    position = lax.axis_index(axis)
    partner = lax.ppermute(block, axis, [(i, (i + ring) % size) for i in range(size)])
    pair = jnp.where(
        position // ring == 0, jnp.stack([block, partner]), jnp.stack([partner, block])
    )
    ring_pos = position % ring
    forward = [(y * ring + a, y * ring + (a + 1) % ring) for y in range(2) for a in range(ring)]
    backward = [(y * ring + a, y * ring + (a - 1) % ring) for y in range(2) for a in range(ring)]
    pieces = [(pair, ring_pos)]
    ahead = pair
    behind = pair
    for step in range(1, ring // 2 + 1):
        ahead = lax.ppermute(ahead, axis, forward)
        pieces.append((ahead, (ring_pos - step) % ring))
        if step < ring - ring // 2:
            behind = lax.ppermute(behind, axis, backward)
            pieces.append((behind, (ring_pos + step) % ring))
    return pieces, ring


def ring_gather(block, axis):
    pieces, ring = ring_pieces(block, axis)
    gathered = jnp.zeros((ring,) + pieces[0][0].shape, block.dtype)
    for piece, source in pieces:
        gathered = lax.dynamic_update_index_in_dim(gathered, piece, source, 0)
    gathered = jnp.swapaxes(gathered, 0, 1)
    return gathered.reshape((2 * ring * block.shape[0],) + block.shape[1:])


def halving_scatter(partial, axis, order):
    size = lax.axis_size(axis)
    position = lax.axis_index(axis)
    state = partial
    for bit in order:
        half = state.shape[1] // 2
        mine = (position >> bit) & 1
        keep = lax.dynamic_slice_in_dim(state, mine * half, half, 1)
        send = lax.dynamic_slice_in_dim(state, (1 - mine) * half, half, 1)
        got = lax.ppermute(
            send.astype(jnp.bfloat16), axis, [(i, i ^ (1 << bit)) for i in range(size)]
        )
        state = keep + got.astype(jnp.float32)
    return state


def attend_piece(state_now, kv_piece, key_frame, queries, query_frame, query_first, head_dim):
    run_max, run_sum, accumulated = state_now
    key_part = kv_piece[:, :, :head_dim]
    value_part = kv_piece[:, :, head_dim:]
    scores = jnp.einsum(
        "nhe,mhe->nhm", queries, key_part, preferred_element_type=jnp.float32
    ) * head_dim ** (-0.5)
    allowed = (key_frame[None, :] <= query_frame[:, None]) & (
        key_frame[None, :] >= query_first[:, None]
    )
    masked = jnp.where(allowed[:, None, :], scores, NEG)
    new_max = jnp.maximum(run_max, masked.max(-1))
    exponent = jnp.where(allowed[:, None, :], jnp.exp(masked - new_max[..., None]), 0.0)
    factor = jnp.exp(run_max - new_max)
    run_sum = run_sum * factor + exponent.sum(-1)
    accumulated = accumulated * factor[..., None] + jnp.einsum(
        "nhm,mhe->nhe",
        exponent.astype(jnp.bfloat16),
        value_part,
        preferred_element_type=jnp.float32,
    )
    return (new_max, run_sum, accumulated)


def per_device(
    latents, timestep, offsets, qkv_weight, mod_weight, gate_weight, out_weight, conv_weight
):
    tok_rows = latents.shape[0]
    heads_here = qkv_weight.shape[1]
    head_dim = out_weight.shape[2]
    chan_here = gate_weight.shape[1]
    frame_size = HH * WW
    frames_here = tok_rows // frame_size
    position = lax.axis_index("ctx")
    column = lax.axis_index("fsdp")
    time_act = time_features(timestep, gate_weight.shape[0])
    gate_vec = jnp.dot(time_act, gate_weight, preferred_element_type=jnp.float32)
    float_rows = latents.astype(jnp.float32)
    centred = float_rows - float_rows.mean(-1, keepdims=True)
    variance = (centred * centred).mean(-1, keepdims=True)
    normed = centred * lax.rsqrt(variance + EPS)

    rows_here = qkv_weight.shape[0]
    qkv_width = qkv_weight.shape[2]
    qkv_cols = heads_here * qkv_width
    out_cols = heads_here * head_dim
    width = qkv_cols + out_cols
    local_shares = jnp.einsum(
        "rjt,t->rj", mod_weight, time_act, preferred_element_type=jnp.float32
    )
    shares_hi = local_shares.astype(jnp.bfloat16)
    shares_lo = (local_shares - shares_hi.astype(jnp.float32)).astype(jnp.bfloat16)
    share_count = 4 * rows_here
    extra_rows = 8 * ((share_count + 8 * width - 1) // (8 * width))
    share_block = jnp.zeros((extra_rows * width,), jnp.bfloat16)
    share_block = share_block.at[:share_count].set(
        jnp.concatenate([shares_hi, shares_lo], axis=1).reshape(share_count)
    )
    bundle = jnp.concatenate(
        [
            jnp.concatenate(
                [
                    qkv_weight.reshape(rows_here, qkv_cols),
                    out_weight.reshape(rows_here, out_cols),
                ],
                axis=1,
            ),
            share_block.reshape(extra_rows, width),
        ],
        axis=0,
    )
    gathered = ring_gather(bundle, "ctx")
    blocks = gathered.shape[0] // bundle.shape[0]
    gathered = gathered.reshape(blocks, rows_here + extra_rows, width)
    full_rows = blocks * rows_here
    w_piece = gathered[:, :rows_here, :qkv_cols].reshape(full_rows, heads_here, qkv_width)
    o_piece = gathered[:, :rows_here, qkv_cols:].reshape(full_rows, heads_here, head_dim)
    share_bits = (
        gathered[:, rows_here:, :]
        .reshape(blocks, extra_rows * width)[:, :share_count]
        .reshape(full_rows, 4)
        .astype(jnp.float32)
    )
    shares = share_bits[:, :2] + share_bits[:, 2:]

    modulated = (normed * (1.0 + shares[:, 1]) + shares[:, 0]).astype(jnp.bfloat16)
    projected_qkv = jnp.einsum(
        "nr,rhc->nhc", modulated, w_piece, preferred_element_type=jnp.float32
    ).astype(jnp.bfloat16)
    queries = projected_qkv[:, :, :head_dim]
    packed = projected_qkv[:, :, head_dim:]
    query_frame = position * frames_here + jnp.arange(tok_rows, dtype=jnp.int32) // frame_size
    local_first = lax.dynamic_slice_in_dim(offsets, position * frames_here, frames_here, 0)
    query_first = jnp.repeat(local_first, frame_size)
    state = (
        jnp.full((tok_rows, heads_here), NEG, jnp.float32),
        jnp.zeros((tok_rows, heads_here), jnp.float32),
        jnp.zeros((tok_rows, heads_here, head_dim), jnp.float32),
    )
    size = lax.axis_size("ctx")
    ring = size // 2
    partner = lax.ppermute(packed, "ctx", [(i, (i + ring) % size) for i in range(size)])
    pair = jnp.where(
        position // ring == 0, jnp.stack([packed, partner]), jnp.stack([partner, packed])
    )
    ring_pos = position % ring
    forward = [(y * ring + a, y * ring + (a + 1) % ring) for y in range(2) for a in range(ring)]
    backward = [(y * ring + a, y * ring + (a - 1) % ring) for y in range(2) for a in range(ring)]
    token_ids = jnp.arange(tok_rows, dtype=jnp.int32)

    def fold(state_in, piece, source):
        key_frame = (
            jnp.concatenate(
                [source * tok_rows + token_ids, (ring + source) * tok_rows + token_ids]
            )
            // frame_size
        )
        return attend_piece(
            state_in,
            piece.reshape((2 * tok_rows,) + piece.shape[2:]),
            key_frame,
            queries,
            query_frame,
            query_first,
            head_dim,
        )

    ahead = pair
    behind = pair
    waiting = [(pair, ring_pos)]
    for step in range(1, ring // 2 + 1):
        ahead, behind, state = lax.optimization_barrier((ahead, behind, state))
        ahead = lax.ppermute(ahead, "ctx", forward)
        arrived = [(ahead, (ring_pos - step) % ring)]
        if step < ring - ring // 2:
            behind = lax.ppermute(behind, "ctx", backward)
            arrived.append((behind, (ring_pos + step) % ring))
        for piece, source in waiting:
            state = fold(state, piece, source)
        waiting = arrived
    for piece, source in waiting:
        state = fold(state, piece, source)
    run_max, run_sum, accumulated = state
    attended = (accumulated / run_sum[..., None]).astype(jnp.bfloat16)
    size = lax.axis_size("fsdp")
    bits = size.bit_length() - 1
    middle = list(range(1, bits - 1))
    half_rows = tok_rows // 2
    orders = [[0, bits - 1] + middle, [0] + middle + [bits - 1]]
    head_parts = []
    for part, order in enumerate(orders):
        by_bit = o_piece.reshape((2,) * bits + (full_rows // size,) + o_piece.shape[1:])
        permuted = jnp.transpose(
            by_bit,
            [bits - 1 - bit for bit in order] + list(range(bits, by_bit.ndim)),
        )
        partial_out = jnp.einsum(
            "nhe,rhe->nr",
            attended[part * half_rows : (part + 1) * half_rows],
            permuted.reshape(o_piece.shape),
            preferred_element_type=jnp.float32,
        )
        head_parts.append(halving_scatter(partial_out, "fsdp", order))
    head_total = jnp.concatenate(head_parts, axis=0)
    own_chan = lax.dynamic_slice_in_dim(latents, column * chan_here, chan_here, 1)
    before = passed_along(own_chan, "ctx", 1)
    stacked = (
        jnp.concatenate([before, own_chan], 0)
        .astype(jnp.float32)
        .reshape(frames_here + 2, HH, WW, chan_here)
    )
    padded = jnp.pad(stacked, ((0, 0), (1, 1), (1, 1), (0, 0)))
    convolved = jnp.zeros((frames_here, HH, WW, chan_here), jnp.float32)
    for time_lag in range(3):
        for row_shift in range(3):
            for col_shift in range(3):
                tap = conv_weight[time_lag, row_shift, col_shift].astype(jnp.float32)
                convolved = (
                    convolved
                    + tap
                    * padded[
                        2 - time_lag : 2 - time_lag + frames_here,
                        row_shift : row_shift + HH,
                        col_shift : col_shift + WW,
                    ]
                )
    residual = own_chan.astype(jnp.float32)
    mixed = residual + gate_vec * head_total + convolved.reshape(tok_rows, chan_here)
    return mixed.astype(jnp.bfloat16)


def solution(mesh):
    in_specs = (
        P("ctx", None),
        P(),
        P(),
        P("ctx", "fsdp", None),
        P("ctx", None, None),
        P(None, "fsdp"),
        P("ctx", "fsdp", None),
        P(None, None, None, "fsdp"),
    )
    out_specs = P("ctx", "fsdp")
    return jax.shard_map(
        per_device, mesh=mesh, in_specs=in_specs, out_specs=out_specs, check_vma=False
    )
```

```python
import math

import jax
import jax.numpy as jnp
from jax import lax
from jax.sharding import PartitionSpec as P

HH = 10
WW = 16


EPS = 1e-06
NEG = -1e30


def passed_along(block, axis, distance):
    devices = range(lax.axis_size(axis))
    route = [(i - distance, i) for i in devices if i - distance in devices]
    return lax.ppermute(block, axis, route)


def time_features(timestep, embed_width):
    half_width = embed_width // 2
    freqs = jnp.exp(-math.log(10000.0) * jnp.arange(half_width, dtype=jnp.float32) / half_width)
    angles = timestep[0].astype(jnp.float32) * freqs
    embed = jnp.concatenate([jnp.cos(angles), jnp.sin(angles)])
    return jax.nn.silu(embed).astype(jnp.bfloat16)


def ring_pieces(block, axis):
    size = lax.axis_size(axis)
    ring = size // 2
    position = lax.axis_index(axis)
    partner = lax.ppermute(block, axis, [(i, (i + ring) % size) for i in range(size)])
    pair = jnp.where(
        position // ring == 0, jnp.stack([block, partner]), jnp.stack([partner, block])
    )
    ring_pos = position % ring
    forward = [(y * ring + a, y * ring + (a + 1) % ring) for y in range(2) for a in range(ring)]
    backward = [(y * ring + a, y * ring + (a - 1) % ring) for y in range(2) for a in range(ring)]
    pieces = [(pair, ring_pos)]
    ahead = pair
    behind = pair
    for step in range(1, ring // 2 + 1):
        ahead = lax.ppermute(ahead, axis, forward)
        pieces.append((ahead, (ring_pos - step) % ring))
        if step < ring - ring // 2:
            behind = lax.ppermute(behind, axis, backward)
            pieces.append((behind, (ring_pos + step) % ring))
    return pieces, ring


def ring_gather(block, axis):
    pieces, ring = ring_pieces(block, axis)
    gathered = jnp.zeros((ring,) + pieces[0][0].shape, block.dtype)
    for piece, source in pieces:
        gathered = lax.dynamic_update_index_in_dim(gathered, piece, source, 0)
    gathered = jnp.swapaxes(gathered, 0, 1)
    return gathered.reshape((2 * ring * block.shape[0],) + block.shape[1:])


def halving_scatter(partial, axis, order):
    size = lax.axis_size(axis)
    position = lax.axis_index(axis)
    state = partial
    for bit in order:
        half = state.shape[1] // 2
        mine = (position >> bit) & 1
        keep = lax.dynamic_slice_in_dim(state, mine * half, half, 1)
        send = lax.dynamic_slice_in_dim(state, (1 - mine) * half, half, 1)
        got = lax.ppermute(
            send.astype(jnp.bfloat16), axis, [(i, i ^ (1 << bit)) for i in range(size)]
        )
        state = keep + got.astype(jnp.float32)
    return state


def attend_piece(state_now, kv_piece, key_frame, queries, query_frame, query_first, head_dim):
    run_max, run_sum, accumulated = state_now
    key_part = kv_piece[:, :, :head_dim]
    value_part = kv_piece[:, :, head_dim:]
    scores = jnp.einsum(
        "nhe,mhe->nhm", queries, key_part, preferred_element_type=jnp.float32
    ) * head_dim ** (-0.5)
    allowed = (key_frame[None, :] <= query_frame[:, None]) & (
        key_frame[None, :] >= query_first[:, None]
    )
    masked = jnp.where(allowed[:, None, :], scores, NEG)
    new_max = jnp.maximum(run_max, masked.max(-1))
    exponent = jnp.where(allowed[:, None, :], jnp.exp(masked - new_max[..., None]), 0.0)
    factor = jnp.exp(run_max - new_max)
    run_sum = run_sum * factor + exponent.sum(-1)
    accumulated = accumulated * factor[..., None] + jnp.einsum(
        "nhm,mhe->nhe",
        exponent.astype(jnp.bfloat16),
        value_part,
        preferred_element_type=jnp.float32,
    )
    return (new_max, run_sum, accumulated)


def per_device(
    latents, timestep, offsets, qkv_weight, mod_weight, gate_weight, out_weight, conv_weight
):
    tok_rows = latents.shape[0]
    heads_here = qkv_weight.shape[1]
    head_dim = out_weight.shape[2]
    chan_here = gate_weight.shape[1]
    frame_size = HH * WW
    frames_here = tok_rows // frame_size
    position = lax.axis_index("ctx")
    column = lax.axis_index("fsdp")
    time_act = time_features(timestep, gate_weight.shape[0])
    gate_vec = jnp.dot(time_act, gate_weight, preferred_element_type=jnp.float32)
    float_rows = latents.astype(jnp.float32)
    centred = float_rows - float_rows.mean(-1, keepdims=True)
    variance = (centred * centred).mean(-1, keepdims=True)
    normed = centred * lax.rsqrt(variance + EPS)

    rows_here = qkv_weight.shape[0]
    qkv_width = qkv_weight.shape[2]
    qkv_cols = heads_here * qkv_width
    out_cols = heads_here * head_dim
    width = qkv_cols + out_cols
    local_shares = jnp.einsum(
        "rjt,t->rj", mod_weight, time_act, preferred_element_type=jnp.float32
    )
    shares_hi = local_shares.astype(jnp.bfloat16)
    shares_lo = (local_shares - shares_hi.astype(jnp.float32)).astype(jnp.bfloat16)
    share_count = 4 * rows_here
    extra_rows = 8 * ((share_count + 8 * width - 1) // (8 * width))
    share_block = jnp.zeros((extra_rows * width,), jnp.bfloat16)
    share_block = share_block.at[:share_count].set(
        jnp.concatenate([shares_hi, shares_lo], axis=1).reshape(share_count)
    )
    bundle = jnp.concatenate(
        [
            jnp.concatenate(
                [
                    qkv_weight.reshape(rows_here, qkv_cols),
                    out_weight.reshape(rows_here, out_cols),
                ],
                axis=1,
            ),
            share_block.reshape(extra_rows, width),
        ],
        axis=0,
    )
    gathered = ring_gather(bundle, "ctx")
    blocks = gathered.shape[0] // bundle.shape[0]
    gathered = gathered.reshape(blocks, rows_here + extra_rows, width)
    full_rows = blocks * rows_here
    w_piece = gathered[:, :rows_here, :qkv_cols].reshape(full_rows, heads_here, qkv_width)
    o_piece = gathered[:, :rows_here, qkv_cols:].reshape(full_rows, heads_here, head_dim)
    share_bits = (
        gathered[:, rows_here:, :]
        .reshape(blocks, extra_rows * width)[:, :share_count]
        .reshape(full_rows, 4)
        .astype(jnp.float32)
    )
    shares = share_bits[:, :2] + share_bits[:, 2:]

    modulated = (normed * (1.0 + shares[:, 1]) + shares[:, 0]).astype(jnp.bfloat16)
    projected_qkv = jnp.einsum(
        "nr,rhc->nhc", modulated, w_piece, preferred_element_type=jnp.float32
    ).astype(jnp.bfloat16)
    queries = projected_qkv[:, :, :head_dim]
    packed = projected_qkv[:, :, head_dim:]
    query_frame = position * frames_here + jnp.arange(tok_rows, dtype=jnp.int32) // frame_size
    local_first = lax.dynamic_slice_in_dim(offsets, position * frames_here, frames_here, 0)
    query_first = jnp.repeat(local_first, frame_size)
    state = (
        jnp.full((tok_rows, heads_here), NEG, jnp.float32),
        jnp.zeros((tok_rows, heads_here), jnp.float32),
        jnp.zeros((tok_rows, heads_here, head_dim), jnp.float32),
    )
    size = lax.axis_size("ctx")
    ring = size // 2
    partner = lax.ppermute(packed, "ctx", [(i, (i + ring) % size) for i in range(size)])
    pair = jnp.where(
        position // ring == 0, jnp.stack([packed, partner]), jnp.stack([partner, packed])
    )
    ring_pos = position % ring
    forward = [(y * ring + a, y * ring + (a + 1) % ring) for y in range(2) for a in range(ring)]
    backward = [(y * ring + a, y * ring + (a - 1) % ring) for y in range(2) for a in range(ring)]
    token_ids = jnp.arange(tok_rows, dtype=jnp.int32)

    def fold(state_in, piece, source):
        key_frame = (
            jnp.concatenate(
                [source * tok_rows + token_ids, (ring + source) * tok_rows + token_ids]
            )
            // frame_size
        )
        return attend_piece(
            state_in,
            piece.reshape((2 * tok_rows,) + piece.shape[2:]),
            key_frame,
            queries,
            query_frame,
            query_first,
            head_dim,
        )

    ahead = pair
    behind = pair
    waiting = [(pair, ring_pos)]
    for step in range(1, ring // 2 + 1):
        ahead, state = lax.optimization_barrier((ahead, state))
        ahead = lax.ppermute(ahead, "ctx", forward)
        arrived = [(ahead, (ring_pos - step) % ring)]
        if step < ring - ring // 2:
            behind = lax.ppermute(behind, "ctx", backward)
            arrived.append((behind, (ring_pos + step) % ring))
        for piece, source in waiting:
            state = fold(state, piece, source)
        waiting = arrived
    for piece, source in waiting:
        state = fold(state, piece, source)
    run_max, run_sum, accumulated = state
    attended = (accumulated / run_sum[..., None]).astype(jnp.bfloat16)
    size = lax.axis_size("fsdp")
    bits = size.bit_length() - 1
    middle = list(range(1, bits - 1))
    half_rows = tok_rows // 2
    orders = [[0, bits - 1] + middle, [0] + middle + [bits - 1]]
    head_parts = []
    for part, order in enumerate(orders):
        by_bit = o_piece.reshape((2,) * bits + (full_rows // size,) + o_piece.shape[1:])
        permuted = jnp.transpose(
            by_bit,
            [bits - 1 - bit for bit in order] + list(range(bits, by_bit.ndim)),
        )
        partial_out = jnp.einsum(
            "nhe,rhe->nr",
            attended[part * half_rows : (part + 1) * half_rows],
            permuted.reshape(o_piece.shape),
            preferred_element_type=jnp.float32,
        )
        head_parts.append(halving_scatter(partial_out, "fsdp", order))
    head_total = jnp.concatenate(head_parts, axis=0)
    own_chan = lax.dynamic_slice_in_dim(latents, column * chan_here, chan_here, 1)
    before = passed_along(own_chan, "ctx", 1)
    stacked = (
        jnp.concatenate([before, own_chan], 0)
        .astype(jnp.float32)
        .reshape(frames_here + 2, HH, WW, chan_here)
    )
    padded = jnp.pad(stacked, ((0, 0), (1, 1), (1, 1), (0, 0)))
    convolved = jnp.zeros((frames_here, HH, WW, chan_here), jnp.float32)
    for time_lag in range(3):
        for row_shift in range(3):
            for col_shift in range(3):
                tap = conv_weight[time_lag, row_shift, col_shift].astype(jnp.float32)
                convolved = (
                    convolved
                    + tap
                    * padded[
                        2 - time_lag : 2 - time_lag + frames_here,
                        row_shift : row_shift + HH,
                        col_shift : col_shift + WW,
                    ]
                )
    residual = own_chan.astype(jnp.float32)
    mixed = residual + gate_vec * head_total + convolved.reshape(tok_rows, chan_here)
    return mixed.astype(jnp.bfloat16)


def solution(mesh):
    in_specs = (
        P("ctx", None),
        P(),
        P(),
        P("ctx", "fsdp", None),
        P("ctx", None, None),
        P(None, "fsdp"),
        P("ctx", "fsdp", None),
        P(None, None, None, "fsdp"),
    )
    out_specs = P("ctx", "fsdp")
    return jax.shard_map(
        per_device, mesh=mesh, in_specs=in_specs, out_specs=out_specs, check_vma=False
    )
```

```python
import math

import jax
import jax.numpy as jnp
from jax import lax
from jax.sharding import PartitionSpec as P

HH = 10
WW = 16


EPS = 1e-06
NEG = -1e30


def passed_along(block, axis, distance):
    devices = range(lax.axis_size(axis))
    route = [(i - distance, i) for i in devices if i - distance in devices]
    return lax.ppermute(block, axis, route)


def time_features(timestep, embed_width):
    half_width = embed_width // 2
    freqs = jnp.exp(-math.log(10000.0) * jnp.arange(half_width, dtype=jnp.float32) / half_width)
    angles = timestep[0].astype(jnp.float32) * freqs
    embed = jnp.concatenate([jnp.cos(angles), jnp.sin(angles)])
    return jax.nn.silu(embed).astype(jnp.bfloat16)


def ring_pieces(block, axis):
    size = lax.axis_size(axis)
    ring = size // 2
    position = lax.axis_index(axis)
    partner = lax.ppermute(block, axis, [(i, (i + ring) % size) for i in range(size)])
    pair = jnp.where(
        position // ring == 0, jnp.stack([block, partner]), jnp.stack([partner, block])
    )
    ring_pos = position % ring
    forward = [(y * ring + a, y * ring + (a + 1) % ring) for y in range(2) for a in range(ring)]
    backward = [(y * ring + a, y * ring + (a - 1) % ring) for y in range(2) for a in range(ring)]
    pieces = [(pair, ring_pos)]
    ahead = pair
    behind = pair
    for step in range(1, ring // 2 + 1):
        ahead = lax.ppermute(ahead, axis, forward)
        pieces.append((ahead, (ring_pos - step) % ring))
        if step < ring - ring // 2:
            behind = lax.ppermute(behind, axis, backward)
            pieces.append((behind, (ring_pos + step) % ring))
    return pieces, ring


def ring_gather(block, axis):
    pieces, ring = ring_pieces(block, axis)
    gathered = jnp.zeros((ring,) + pieces[0][0].shape, block.dtype)
    for piece, source in pieces:
        gathered = lax.dynamic_update_index_in_dim(gathered, piece, source, 0)
    gathered = jnp.swapaxes(gathered, 0, 1)
    return gathered.reshape((2 * ring * block.shape[0],) + block.shape[1:])


def halving_scatter(parts, axis, orders):
    size = lax.axis_size(axis)
    position = lax.axis_index(axis)
    states = list(parts)
    for stage in range(len(orders[0])):
        keeps = []
        sends = []
        for index, state in enumerate(states):
            bit = orders[index][stage]
            half = state.shape[1] // 2
            mine = (position >> bit) & 1
            keeps.append(lax.dynamic_slice_in_dim(state, mine * half, half, 1))
            sends.append(lax.dynamic_slice_in_dim(state, (1 - mine) * half, half, 1))
        stage_bits = [order[stage] for order in orders]
        if len(set(stage_bits)) == 1:
            bit = stage_bits[0]
            joined = lax.ppermute(
                jnp.concatenate(sends, axis=0).astype(jnp.bfloat16),
                axis,
                [(i, i ^ (1 << bit)) for i in range(size)],
            )
            bounds = [0]
            for send in sends:
                bounds.append(bounds[-1] + send.shape[0])
            got = [joined[bounds[i] : bounds[i + 1]] for i in range(len(sends))]
        else:
            got = [
                lax.ppermute(
                    send.astype(jnp.bfloat16),
                    axis,
                    [(i, i ^ (1 << bit)) for i in range(size)],
                )
                for send, bit in zip(sends, stage_bits)
            ]
        states = [keep + g.astype(jnp.float32) for keep, g in zip(keeps, got)]
    return states


def attend_piece(state_now, kv_piece, key_frame, queries, query_frame, query_first, head_dim):
    run_max, run_sum, accumulated = state_now
    key_part = kv_piece[:, :, :head_dim]
    value_part = kv_piece[:, :, head_dim:]
    scores = jnp.einsum(
        "nhe,mhe->nhm", queries, key_part, preferred_element_type=jnp.float32
    ) * head_dim ** (-0.5)
    allowed = (key_frame[None, :] <= query_frame[:, None]) & (
        key_frame[None, :] >= query_first[:, None]
    )
    masked = jnp.where(allowed[:, None, :], scores, NEG)
    new_max = jnp.maximum(run_max, masked.max(-1))
    exponent = jnp.where(allowed[:, None, :], jnp.exp(masked - new_max[..., None]), 0.0)
    factor = jnp.exp(run_max - new_max)
    run_sum = run_sum * factor + exponent.sum(-1)
    accumulated = accumulated * factor[..., None] + jnp.einsum(
        "nhm,mhe->nhe",
        exponent.astype(jnp.bfloat16),
        value_part,
        preferred_element_type=jnp.float32,
    )
    return (new_max, run_sum, accumulated)


def per_device(
    latents, timestep, offsets, qkv_weight, mod_weight, gate_weight, out_weight, conv_weight
):
    tok_rows = latents.shape[0]
    heads_here = qkv_weight.shape[1]
    head_dim = out_weight.shape[2]
    chan_here = gate_weight.shape[1]
    frame_size = HH * WW
    frames_here = tok_rows // frame_size
    position = lax.axis_index("ctx")
    column = lax.axis_index("fsdp")
    time_act = time_features(timestep, gate_weight.shape[0])
    gate_vec = jnp.dot(time_act, gate_weight, preferred_element_type=jnp.float32)
    float_rows = latents.astype(jnp.float32)
    centred = float_rows - float_rows.mean(-1, keepdims=True)
    variance = (centred * centred).mean(-1, keepdims=True)
    normed = centred * lax.rsqrt(variance + EPS)

    rows_here = qkv_weight.shape[0]
    qkv_width = qkv_weight.shape[2]
    qkv_cols = heads_here * qkv_width
    out_cols = heads_here * head_dim
    width = qkv_cols + out_cols
    local_shares = jnp.einsum(
        "rjt,t->rj", mod_weight, time_act, preferred_element_type=jnp.float32
    )
    shares_hi = local_shares.astype(jnp.bfloat16)
    shares_lo = (local_shares - shares_hi.astype(jnp.float32)).astype(jnp.bfloat16)
    share_count = 4 * rows_here
    extra_rows = 8 * ((share_count + 8 * width - 1) // (8 * width))
    share_block = jnp.zeros((extra_rows * width,), jnp.bfloat16)
    share_block = share_block.at[:share_count].set(
        jnp.concatenate([shares_hi, shares_lo], axis=1).reshape(share_count)
    )
    bundle = jnp.concatenate(
        [
            jnp.concatenate(
                [
                    qkv_weight.reshape(rows_here, qkv_cols),
                    out_weight.reshape(rows_here, out_cols),
                ],
                axis=1,
            ),
            share_block.reshape(extra_rows, width),
        ],
        axis=0,
    )
    gathered = ring_gather(bundle, "ctx")
    blocks = gathered.shape[0] // bundle.shape[0]
    gathered = gathered.reshape(blocks, rows_here + extra_rows, width)
    full_rows = blocks * rows_here
    w_piece = gathered[:, :rows_here, :qkv_cols].reshape(full_rows, heads_here, qkv_width)
    o_piece = gathered[:, :rows_here, qkv_cols:].reshape(full_rows, heads_here, head_dim)
    share_bits = (
        gathered[:, rows_here:, :]
        .reshape(blocks, extra_rows * width)[:, :share_count]
        .reshape(full_rows, 4)
        .astype(jnp.float32)
    )
    shares = share_bits[:, :2] + share_bits[:, 2:]

    modulated = (normed * (1.0 + shares[:, 1]) + shares[:, 0]).astype(jnp.bfloat16)
    projected_qkv = jnp.einsum(
        "nr,rhc->nhc", modulated, w_piece, preferred_element_type=jnp.float32
    ).astype(jnp.bfloat16)
    queries = projected_qkv[:, :, :head_dim]
    packed = projected_qkv[:, :, head_dim:]
    query_frame = position * frames_here + jnp.arange(tok_rows, dtype=jnp.int32) // frame_size
    local_first = lax.dynamic_slice_in_dim(offsets, position * frames_here, frames_here, 0)
    query_first = jnp.repeat(local_first, frame_size)
    state = (
        jnp.full((tok_rows, heads_here), NEG, jnp.float32),
        jnp.zeros((tok_rows, heads_here), jnp.float32),
        jnp.zeros((tok_rows, heads_here, head_dim), jnp.float32),
    )
    size = lax.axis_size("ctx")
    ring = size // 2
    partner = lax.ppermute(packed, "ctx", [(i, (i + ring) % size) for i in range(size)])
    pair = jnp.where(
        position // ring == 0, jnp.stack([packed, partner]), jnp.stack([partner, packed])
    )
    ring_pos = position % ring
    forward = [(y * ring + a, y * ring + (a + 1) % ring) for y in range(2) for a in range(ring)]
    backward = [(y * ring + a, y * ring + (a - 1) % ring) for y in range(2) for a in range(ring)]
    token_ids = jnp.arange(tok_rows, dtype=jnp.int32)

    def fold(state_in, piece, source):
        key_frame = (
            jnp.concatenate(
                [source * tok_rows + token_ids, (ring + source) * tok_rows + token_ids]
            )
            // frame_size
        )
        return attend_piece(
            state_in,
            piece.reshape((2 * tok_rows,) + piece.shape[2:]),
            key_frame,
            queries,
            query_frame,
            query_first,
            head_dim,
        )

    ahead = pair
    behind = pair
    waiting = [(pair, ring_pos)]
    for step in range(1, ring // 2 + 1):
        ahead, state = lax.optimization_barrier((ahead, state))
        ahead = lax.ppermute(ahead, "ctx", forward)
        arrived = [(ahead, (ring_pos - step) % ring)]
        if step < ring - ring // 2:
            behind = lax.ppermute(behind, "ctx", backward)
            arrived.append((behind, (ring_pos + step) % ring))
        for piece, source in waiting:
            state = fold(state, piece, source)
        waiting = arrived
    for piece, source in waiting:
        state = fold(state, piece, source)
    run_max, run_sum, accumulated = state
    attended = (accumulated / run_sum[..., None]).astype(jnp.bfloat16)
    size = lax.axis_size("fsdp")
    bits = size.bit_length() - 1
    middle = list(range(1, bits - 1))
    half_rows = tok_rows // 2
    if bits == 4:
        orders = [[0, 3, 1, 2], [0, 1, 3, 2]]
    else:
        orders = [[0, bits - 1] + middle, [0] + middle + [bits - 1]]
    partials = []
    for part, order in enumerate(orders):
        by_bit = o_piece.reshape((2,) * bits + (full_rows // size,) + o_piece.shape[1:])
        permuted = jnp.transpose(
            by_bit,
            [bits - 1 - bit for bit in order] + list(range(bits, by_bit.ndim)),
        )
        partials.append(
            jnp.einsum(
                "nhe,rhe->nr",
                attended[part * half_rows : (part + 1) * half_rows],
                permuted.reshape(o_piece.shape),
                preferred_element_type=jnp.float32,
            )
        )
    head_parts = halving_scatter(partials, "fsdp", orders)
    head_total = jnp.concatenate(head_parts, axis=0)
    own_chan = lax.dynamic_slice_in_dim(latents, column * chan_here, chan_here, 1)
    before = passed_along(own_chan, "ctx", 1)
    stacked = (
        jnp.concatenate([before, own_chan], 0)
        .astype(jnp.float32)
        .reshape(frames_here + 2, HH, WW, chan_here)
    )
    padded = jnp.pad(stacked, ((0, 0), (1, 1), (1, 1), (0, 0)))
    convolved = jnp.zeros((frames_here, HH, WW, chan_here), jnp.float32)
    for time_lag in range(3):
        for row_shift in range(3):
            for col_shift in range(3):
                tap = conv_weight[time_lag, row_shift, col_shift].astype(jnp.float32)
                convolved = (
                    convolved
                    + tap
                    * padded[
                        2 - time_lag : 2 - time_lag + frames_here,
                        row_shift : row_shift + HH,
                        col_shift : col_shift + WW,
                    ]
                )
    residual = own_chan.astype(jnp.float32)
    mixed = residual + gate_vec * head_total + convolved.reshape(tok_rows, chan_here)
    return mixed.astype(jnp.bfloat16)


def solution(mesh):
    in_specs = (
        P("ctx", None),
        P(),
        P(),
        P("ctx", "fsdp", None),
        P("ctx", None, None),
        P(None, "fsdp"),
        P("ctx", "fsdp", None),
        P(None, None, None, "fsdp"),
    )
    out_specs = P("ctx", "fsdp")
    return jax.shard_map(
        per_device, mesh=mesh, in_specs=in_specs, out_specs=out_specs, check_vma=False
    )
```

```python
import math

import jax
import jax.numpy as jnp
from jax import lax
from jax.sharding import PartitionSpec as P

HH = 10
WW = 16


EPS = 1e-06
NEG = -1e30


def passed_along(block, axis, distance):
    devices = range(lax.axis_size(axis))
    route = [(i - distance, i) for i in devices if i - distance in devices]
    return lax.ppermute(block, axis, route)


def time_features(timestep, embed_width):
    half_width = embed_width // 2
    freqs = jnp.exp(-math.log(10000.0) * jnp.arange(half_width, dtype=jnp.float32) / half_width)
    angles = timestep[0].astype(jnp.float32) * freqs
    embed = jnp.concatenate([jnp.cos(angles), jnp.sin(angles)])
    return jax.nn.silu(embed).astype(jnp.bfloat16)


def ring_pieces(block, axis):
    size = lax.axis_size(axis)
    ring = size // 2
    position = lax.axis_index(axis)
    partner = lax.ppermute(block, axis, [(i, (i + ring) % size) for i in range(size)])
    pair = jnp.where(
        position // ring == 0, jnp.stack([block, partner]), jnp.stack([partner, block])
    )
    ring_pos = position % ring
    forward = [(y * ring + a, y * ring + (a + 1) % ring) for y in range(2) for a in range(ring)]
    backward = [(y * ring + a, y * ring + (a - 1) % ring) for y in range(2) for a in range(ring)]
    pieces = [(pair, ring_pos, (0, 1))]
    ahead = pair
    behind = pair
    for step in range(1, ring // 2 + 1):
        source = (ring_pos - step) % ring
        if 2 * step == ring:
            ahead = lax.ppermute(ahead[:1], axis, forward)
            behind = lax.ppermute(behind[1:], axis, backward)
            pieces.append((ahead, source, (0,)))
            pieces.append((behind, source, (1,)))
            break
        ahead = lax.ppermute(ahead, axis, forward)
        pieces.append((ahead, source, (0, 1)))
        if step < ring - ring // 2:
            behind = lax.ppermute(behind, axis, backward)
            pieces.append((behind, (ring_pos + step) % ring, (0, 1)))
    return pieces, ring


def ring_gather(block, axis):
    pieces, ring = ring_pieces(block, axis)
    gathered = jnp.zeros((ring,) + pieces[0][0].shape, block.dtype)
    zero = jnp.zeros((), jnp.int32)
    for piece, source, halves in pieces:
        gathered = lax.dynamic_update_slice(
            gathered, piece[None], (source, halves[0]) + (zero,) * block.ndim
        )
    gathered = jnp.swapaxes(gathered, 0, 1)
    return gathered.reshape((2 * ring * block.shape[0],) + block.shape[1:])


def halving_scatter(partial, axis, order):
    size = lax.axis_size(axis)
    position = lax.axis_index(axis)
    state = partial
    for bit in order:
        half = state.shape[1] // 2
        mine = (position >> bit) & 1
        keep = lax.dynamic_slice_in_dim(state, mine * half, half, 1)
        send = lax.dynamic_slice_in_dim(state, (1 - mine) * half, half, 1)
        got = lax.ppermute(
            send.astype(jnp.bfloat16), axis, [(i, i ^ (1 << bit)) for i in range(size)]
        )
        state = keep + got.astype(jnp.float32)
    return state


def attend_piece(state_now, kv_piece, key_frame, queries, query_frame, query_first, head_dim):
    run_max, run_sum, accumulated = state_now
    key_part = kv_piece[:, :, :head_dim]
    value_part = kv_piece[:, :, head_dim:]
    scores = jnp.einsum(
        "nhe,mhe->nhm", queries, key_part, preferred_element_type=jnp.float32
    ) * head_dim ** (-0.5)
    allowed = (key_frame[None, :] <= query_frame[:, None]) & (
        key_frame[None, :] >= query_first[:, None]
    )
    masked = jnp.where(allowed[:, None, :], scores, NEG)
    new_max = jnp.maximum(run_max, masked.max(-1))
    exponent = jnp.where(allowed[:, None, :], jnp.exp(masked - new_max[..., None]), 0.0)
    factor = jnp.exp(run_max - new_max)
    run_sum = run_sum * factor + exponent.sum(-1)
    accumulated = accumulated * factor[..., None] + jnp.einsum(
        "nhm,mhe->nhe",
        exponent.astype(jnp.bfloat16),
        value_part,
        preferred_element_type=jnp.float32,
    )
    return (new_max, run_sum, accumulated)


def per_device(
    latents, timestep, offsets, qkv_weight, mod_weight, gate_weight, out_weight, conv_weight
):
    tok_rows = latents.shape[0]
    heads_here = qkv_weight.shape[1]
    head_dim = out_weight.shape[2]
    chan_here = gate_weight.shape[1]
    frame_size = HH * WW
    frames_here = tok_rows // frame_size
    position = lax.axis_index("ctx")
    column = lax.axis_index("fsdp")
    time_act = time_features(timestep, gate_weight.shape[0])
    gate_vec = jnp.dot(time_act, gate_weight, preferred_element_type=jnp.float32)
    float_rows = latents.astype(jnp.float32)
    centred = float_rows - float_rows.mean(-1, keepdims=True)
    variance = (centred * centred).mean(-1, keepdims=True)
    normed = centred * lax.rsqrt(variance + EPS)

    rows_here = qkv_weight.shape[0]
    qkv_width = qkv_weight.shape[2]
    qkv_cols = heads_here * qkv_width
    out_cols = heads_here * head_dim
    width = qkv_cols + out_cols
    local_shares = jnp.einsum(
        "rjt,t->rj", mod_weight, time_act, preferred_element_type=jnp.float32
    )
    shares_hi = local_shares.astype(jnp.bfloat16)
    shares_lo = (local_shares - shares_hi.astype(jnp.float32)).astype(jnp.bfloat16)
    share_count = 4 * rows_here
    extra_rows = 8 * ((share_count + 8 * width - 1) // (8 * width))
    share_block = jnp.zeros((extra_rows * width,), jnp.bfloat16)
    share_block = share_block.at[:share_count].set(
        jnp.concatenate([shares_hi, shares_lo], axis=1).reshape(share_count)
    )
    bundle = jnp.concatenate(
        [
            jnp.concatenate(
                [
                    qkv_weight.reshape(rows_here, qkv_cols),
                    out_weight.reshape(rows_here, out_cols),
                ],
                axis=1,
            ),
            share_block.reshape(extra_rows, width),
        ],
        axis=0,
    )
    gathered = ring_gather(bundle, "ctx")
    blocks = gathered.shape[0] // bundle.shape[0]
    gathered = gathered.reshape(blocks, rows_here + extra_rows, width)
    full_rows = blocks * rows_here
    w_piece = gathered[:, :rows_here, :qkv_cols].reshape(full_rows, heads_here, qkv_width)
    o_piece = gathered[:, :rows_here, qkv_cols:].reshape(full_rows, heads_here, head_dim)
    share_bits = (
        gathered[:, rows_here:, :]
        .reshape(blocks, extra_rows * width)[:, :share_count]
        .reshape(full_rows, 4)
        .astype(jnp.float32)
    )
    shares = share_bits[:, :2] + share_bits[:, 2:]

    modulated = (normed * (1.0 + shares[:, 1]) + shares[:, 0]).astype(jnp.bfloat16)
    projected_qkv = jnp.einsum(
        "nr,rhc->nhc", modulated, w_piece, preferred_element_type=jnp.float32
    ).astype(jnp.bfloat16)
    queries = projected_qkv[:, :, :head_dim]
    packed = projected_qkv[:, :, head_dim:]
    query_frame = position * frames_here + jnp.arange(tok_rows, dtype=jnp.int32) // frame_size
    local_first = lax.dynamic_slice_in_dim(offsets, position * frames_here, frames_here, 0)
    query_first = jnp.repeat(local_first, frame_size)
    state = (
        jnp.full((tok_rows, heads_here), NEG, jnp.float32),
        jnp.zeros((tok_rows, heads_here), jnp.float32),
        jnp.zeros((tok_rows, heads_here, head_dim), jnp.float32),
    )
    size = lax.axis_size("ctx")
    ring = size // 2
    partner = lax.ppermute(packed, "ctx", [(i, (i + ring) % size) for i in range(size)])
    pair = jnp.where(
        position // ring == 0, jnp.stack([packed, partner]), jnp.stack([partner, packed])
    )
    ring_pos = position % ring
    forward = [(y * ring + a, y * ring + (a + 1) % ring) for y in range(2) for a in range(ring)]
    backward = [(y * ring + a, y * ring + (a - 1) % ring) for y in range(2) for a in range(ring)]
    token_ids = jnp.arange(tok_rows, dtype=jnp.int32)

    def fold(state_in, piece, source, halves):
        key_frame = (
            jnp.concatenate([(half * ring + source) * tok_rows + token_ids for half in halves])
            // frame_size
        )
        return attend_piece(
            state_in,
            piece.reshape((len(halves) * tok_rows,) + piece.shape[2:]),
            key_frame,
            queries,
            query_frame,
            query_first,
            head_dim,
        )

    ahead = pair
    behind = pair
    waiting = [(pair, ring_pos, (0, 1))]
    for step in range(1, ring // 2 + 1):
        ahead, state = lax.optimization_barrier((ahead, state))
        source = (ring_pos - step) % ring
        if 2 * step == ring:
            ahead = lax.ppermute(ahead[:1], "ctx", forward)
            behind = lax.ppermute(behind[1:], "ctx", backward)
            arrived = [(ahead, source, (0,)), (behind, source, (1,))]
        else:
            ahead = lax.ppermute(ahead, "ctx", forward)
            arrived = [(ahead, source, (0, 1))]
            if step < ring - ring // 2:
                behind = lax.ppermute(behind, "ctx", backward)
                arrived.append((behind, (ring_pos + step) % ring, (0, 1)))
        for piece, where, halves in waiting:
            state = fold(state, piece, where, halves)
        waiting = arrived
    for piece, where, halves in waiting:
        state = fold(state, piece, where, halves)
    run_max, run_sum, accumulated = state
    attended = (accumulated / run_sum[..., None]).astype(jnp.bfloat16)
    size = lax.axis_size("fsdp")
    bits = size.bit_length() - 1
    middle = list(range(1, bits - 1))
    half_rows = tok_rows // 2
    orders = [[0, bits - 1] + middle, [0] + middle + [bits - 1]]
    head_parts = []
    for part, order in enumerate(orders):
        by_bit = o_piece.reshape((2,) * bits + (full_rows // size,) + o_piece.shape[1:])
        permuted = jnp.transpose(
            by_bit,
            [bits - 1 - bit for bit in order] + list(range(bits, by_bit.ndim)),
        )
        partial_out = jnp.einsum(
            "nhe,rhe->nr",
            attended[part * half_rows : (part + 1) * half_rows],
            permuted.reshape(o_piece.shape),
            preferred_element_type=jnp.float32,
        )
        head_parts.append(halving_scatter(partial_out, "fsdp", order))
    head_total = jnp.concatenate(head_parts, axis=0)
    own_chan = lax.dynamic_slice_in_dim(latents, column * chan_here, chan_here, 1)
    before = passed_along(own_chan, "ctx", 1)
    stacked = (
        jnp.concatenate([before, own_chan], 0)
        .astype(jnp.float32)
        .reshape(frames_here + 2, HH, WW, chan_here)
    )
    padded = jnp.pad(stacked, ((0, 0), (1, 1), (1, 1), (0, 0)))
    convolved = jnp.zeros((frames_here, HH, WW, chan_here), jnp.float32)
    for time_lag in range(3):
        for row_shift in range(3):
            for col_shift in range(3):
                tap = conv_weight[time_lag, row_shift, col_shift].astype(jnp.float32)
                convolved = (
                    convolved
                    + tap
                    * padded[
                        2 - time_lag : 2 - time_lag + frames_here,
                        row_shift : row_shift + HH,
                        col_shift : col_shift + WW,
                    ]
                )
    residual = own_chan.astype(jnp.float32)
    mixed = residual + gate_vec * head_total + convolved.reshape(tok_rows, chan_here)
    return mixed.astype(jnp.bfloat16)


def solution(mesh):
    in_specs = (
        P("ctx", None),
        P(),
        P(),
        P("ctx", "fsdp", None),
        P("ctx", None, None),
        P(None, "fsdp"),
        P("ctx", "fsdp", None),
        P(None, None, None, "fsdp"),
    )
    out_specs = P("ctx", "fsdp")
    return jax.shard_map(
        per_device, mesh=mesh, in_specs=in_specs, out_specs=out_specs, check_vma=False
    )
```

```python
import math

import jax
import jax.numpy as jnp
from jax import lax
from jax.sharding import PartitionSpec as P

HH = 10
WW = 16


EPS = 1e-06
NEG = -1e30


def passed_along(block, axis, distance):
    devices = range(lax.axis_size(axis))
    route = [(i - distance, i) for i in devices if i - distance in devices]
    return lax.ppermute(block, axis, route)


def time_features(timestep, embed_width):
    half_width = embed_width // 2
    freqs = jnp.exp(-math.log(10000.0) * jnp.arange(half_width, dtype=jnp.float32) / half_width)
    angles = timestep[0].astype(jnp.float32) * freqs
    embed = jnp.concatenate([jnp.cos(angles), jnp.sin(angles)])
    return jax.nn.silu(embed).astype(jnp.bfloat16)


def ring_pieces(block, axis):
    size = lax.axis_size(axis)
    ring = size // 2
    position = lax.axis_index(axis)
    partner = lax.ppermute(block, axis, [(i, (i + ring) % size) for i in range(size)])
    pair = jnp.where(
        position // ring == 0, jnp.stack([block, partner]), jnp.stack([partner, block])
    )
    ring_pos = position % ring
    forward = [(y * ring + a, y * ring + (a + 1) % ring) for y in range(2) for a in range(ring)]
    backward = [(y * ring + a, y * ring + (a - 1) % ring) for y in range(2) for a in range(ring)]
    pieces = [(pair, ring_pos, (0, 1))]
    ahead = pair
    behind = pair
    for step in range(1, ring // 2 + 1):
        source = (ring_pos - step) % ring
        if 2 * step == ring:
            ahead = lax.ppermute(ahead[:1], axis, forward)
            behind = lax.ppermute(behind[1:], axis, backward)
            pieces.append((ahead, source, (0,)))
            pieces.append((behind, source, (1,)))
            break
        ahead = lax.ppermute(ahead, axis, forward)
        pieces.append((ahead, source, (0, 1)))
        if step < ring - ring // 2:
            behind = lax.ppermute(behind, axis, backward)
            pieces.append((behind, (ring_pos + step) % ring, (0, 1)))
    return pieces, ring


def ring_gather(block, axis):
    pieces, ring = ring_pieces(block, axis)
    gathered = jnp.zeros((ring,) + pieces[0][0].shape, block.dtype)
    zero = jnp.zeros((), jnp.int32)
    for piece, source, halves in pieces:
        gathered = lax.dynamic_update_slice(
            gathered, piece[None], (source, halves[0]) + (zero,) * block.ndim
        )
    gathered = jnp.swapaxes(gathered, 0, 1)
    return gathered.reshape((2 * ring * block.shape[0],) + block.shape[1:])


def halving_scatter(partial, axis, order):
    size = lax.axis_size(axis)
    position = lax.axis_index(axis)
    state = partial
    for bit in order:
        half = state.shape[1] // 2
        mine = (position >> bit) & 1
        keep = lax.dynamic_slice_in_dim(state, mine * half, half, 1)
        send = lax.dynamic_slice_in_dim(state, (1 - mine) * half, half, 1)
        got = lax.ppermute(
            send.astype(jnp.bfloat16), axis, [(i, i ^ (1 << bit)) for i in range(size)]
        )
        state = keep + got.astype(jnp.float32)
    return state


def attend_piece(state_now, kv_piece, key_frame, queries, query_frame, query_first, head_dim):
    run_max, run_sum, accumulated = state_now
    key_part = kv_piece[:, :, :head_dim]
    value_part = kv_piece[:, :, head_dim:]
    scores = jnp.einsum(
        "nhe,mhe->nhm", queries, key_part, preferred_element_type=jnp.float32
    ) * head_dim ** (-0.5)
    allowed = (key_frame[None, :] <= query_frame[:, None]) & (
        key_frame[None, :] >= query_first[:, None]
    )
    masked = jnp.where(allowed[:, None, :], scores, NEG)
    new_max = jnp.maximum(run_max, masked.max(-1))
    exponent = jnp.where(allowed[:, None, :], jnp.exp(masked - new_max[..., None]), 0.0)
    factor = jnp.exp(run_max - new_max)
    run_sum = run_sum * factor + exponent.sum(-1)
    accumulated = accumulated * factor[..., None] + jnp.einsum(
        "nhm,mhe->nhe",
        exponent.astype(jnp.bfloat16),
        value_part,
        preferred_element_type=jnp.float32,
    )
    return (new_max, run_sum, accumulated)


def per_device(
    latents, timestep, offsets, qkv_weight, mod_weight, gate_weight, out_weight, conv_weight
):
    tok_rows = latents.shape[0]
    heads_here = qkv_weight.shape[1]
    head_dim = out_weight.shape[2]
    chan_here = gate_weight.shape[1]
    frame_size = HH * WW
    frames_here = tok_rows // frame_size
    position = lax.axis_index("ctx")
    column = lax.axis_index("fsdp")
    time_act = time_features(timestep, gate_weight.shape[0])
    gate_vec = jnp.dot(time_act, gate_weight, preferred_element_type=jnp.float32)
    float_rows = latents.astype(jnp.float32)
    centred = float_rows - float_rows.mean(-1, keepdims=True)
    variance = (centred * centred).mean(-1, keepdims=True)
    normed = centred * lax.rsqrt(variance + EPS)

    rows_here = qkv_weight.shape[0]
    qkv_width = qkv_weight.shape[2]
    qkv_cols = heads_here * qkv_width
    out_cols = heads_here * head_dim
    width = qkv_cols + out_cols
    local_shares = jnp.einsum(
        "rjt,t->rj", mod_weight, time_act, preferred_element_type=jnp.float32
    )
    shares_hi = local_shares.astype(jnp.bfloat16)
    shares_lo = (local_shares - shares_hi.astype(jnp.float32)).astype(jnp.bfloat16)
    share_count = 4 * rows_here
    extra_rows = 8 * ((share_count + 8 * width - 1) // (8 * width))
    share_block = jnp.zeros((extra_rows * width,), jnp.bfloat16)
    share_block = share_block.at[:share_count].set(
        jnp.concatenate([shares_hi, shares_lo], axis=1).reshape(share_count)
    )
    bundle = jnp.concatenate(
        [
            jnp.concatenate(
                [
                    qkv_weight.reshape(rows_here, qkv_cols),
                    out_weight.reshape(rows_here, out_cols),
                ],
                axis=1,
            ),
            share_block.reshape(extra_rows, width),
        ],
        axis=0,
    )
    gathered = ring_gather(bundle, "ctx")
    blocks = gathered.shape[0] // bundle.shape[0]
    gathered = gathered.reshape(blocks, rows_here + extra_rows, width)
    full_rows = blocks * rows_here
    w_piece = gathered[:, :rows_here, :qkv_cols].reshape(full_rows, heads_here, qkv_width)
    o_piece = gathered[:, :rows_here, qkv_cols:].reshape(full_rows, heads_here, head_dim)
    share_bits = (
        gathered[:, rows_here:, :]
        .reshape(blocks, extra_rows * width)[:, :share_count]
        .reshape(full_rows, 4)
        .astype(jnp.float32)
    )
    shares = share_bits[:, :2] + share_bits[:, 2:]

    modulated = (normed * (1.0 + shares[:, 1]) + shares[:, 0]).astype(jnp.bfloat16)
    projected_qkv = jnp.einsum(
        "nr,rhc->nhc", modulated, w_piece, preferred_element_type=jnp.float32
    ).astype(jnp.bfloat16)
    queries = projected_qkv[:, :, :head_dim]
    packed = projected_qkv[:, :, head_dim:]
    query_frame = position * frames_here + jnp.arange(tok_rows, dtype=jnp.int32) // frame_size
    local_first = lax.dynamic_slice_in_dim(offsets, position * frames_here, frames_here, 0)
    query_first = jnp.repeat(local_first, frame_size)
    state = (
        jnp.full((tok_rows, heads_here), NEG, jnp.float32),
        jnp.zeros((tok_rows, heads_here), jnp.float32),
        jnp.zeros((tok_rows, heads_here, head_dim), jnp.float32),
    )
    size = lax.axis_size("ctx")
    ring = size // 2
    partner = lax.ppermute(packed, "ctx", [(i, (i + ring) % size) for i in range(size)])
    pair = jnp.where(
        position // ring == 0, jnp.stack([packed, partner]), jnp.stack([partner, packed])
    )
    ring_pos = position % ring
    forward = [(y * ring + a, y * ring + (a + 1) % ring) for y in range(2) for a in range(ring)]
    backward = [(y * ring + a, y * ring + (a - 1) % ring) for y in range(2) for a in range(ring)]
    token_ids = jnp.arange(tok_rows, dtype=jnp.int32)

    def fold(state_in, piece, source):
        key_frame = (
            jnp.concatenate(
                [source * tok_rows + token_ids, (ring + source) * tok_rows + token_ids]
            )
            // frame_size
        )
        return attend_piece(
            state_in,
            piece.reshape((2 * tok_rows,) + piece.shape[2:]),
            key_frame,
            queries,
            query_frame,
            query_first,
            head_dim,
        )

    ahead = pair
    behind = pair
    waiting = [(pair, ring_pos)]
    for step in range(1, ring // 2 + 1):
        ahead, state = lax.optimization_barrier((ahead, state))
        ahead = lax.ppermute(ahead, "ctx", forward)
        arrived = [(ahead, (ring_pos - step) % ring)]
        if step < ring - ring // 2:
            behind = lax.ppermute(behind, "ctx", backward)
            arrived.append((behind, (ring_pos + step) % ring))
        for piece, source in waiting:
            state = fold(state, piece, source)
        waiting = arrived
    for piece, source in waiting:
        state = fold(state, piece, source)
    run_max, run_sum, accumulated = state
    attended = (accumulated / run_sum[..., None]).astype(jnp.bfloat16)
    size = lax.axis_size("fsdp")
    bits = size.bit_length() - 1
    middle = list(range(1, bits - 1))
    half_rows = tok_rows // 2
    orders = [[0, bits - 1] + middle, [0] + middle + [bits - 1]]
    head_parts = []
    for part, order in enumerate(orders):
        by_bit = o_piece.reshape((2,) * bits + (full_rows // size,) + o_piece.shape[1:])
        permuted = jnp.transpose(
            by_bit,
            [bits - 1 - bit for bit in order] + list(range(bits, by_bit.ndim)),
        )
        partial_out = jnp.einsum(
            "nhe,rhe->nr",
            attended[part * half_rows : (part + 1) * half_rows],
            permuted.reshape(o_piece.shape),
            preferred_element_type=jnp.float32,
        )
        head_parts.append(halving_scatter(partial_out, "fsdp", order))
    head_total = jnp.concatenate(head_parts, axis=0)
    own_chan = lax.dynamic_slice_in_dim(latents, column * chan_here, chan_here, 1)
    before = passed_along(own_chan, "ctx", 1)
    stacked = (
        jnp.concatenate([before, own_chan], 0)
        .astype(jnp.float32)
        .reshape(frames_here + 2, HH, WW, chan_here)
    )
    padded = jnp.pad(stacked, ((0, 0), (1, 1), (1, 1), (0, 0)))
    convolved = jnp.zeros((frames_here, HH, WW, chan_here), jnp.float32)
    for time_lag in range(3):
        for row_shift in range(3):
            for col_shift in range(3):
                tap = conv_weight[time_lag, row_shift, col_shift].astype(jnp.float32)
                convolved = (
                    convolved
                    + tap
                    * padded[
                        2 - time_lag : 2 - time_lag + frames_here,
                        row_shift : row_shift + HH,
                        col_shift : col_shift + WW,
                    ]
                )
    residual = own_chan.astype(jnp.float32)
    mixed = residual + gate_vec * head_total + convolved.reshape(tok_rows, chan_here)
    return mixed.astype(jnp.bfloat16)


def solution(mesh):
    in_specs = (
        P("ctx", None),
        P(),
        P(),
        P("ctx", "fsdp", None),
        P("ctx", None, None),
        P(None, "fsdp"),
        P("ctx", "fsdp", None),
        P(None, None, None, "fsdp"),
    )
    out_specs = P("ctx", "fsdp")
    return jax.shard_map(
        per_device, mesh=mesh, in_specs=in_specs, out_specs=out_specs, check_vma=False
    )
```

```python
import math

import jax
import jax.numpy as jnp
from jax import lax
from jax.sharding import PartitionSpec as P

HH = 10
WW = 16


EPS = 1e-06
NEG = -1e30


def passed_along(block, axis, distance):
    devices = range(lax.axis_size(axis))
    route = [(i - distance, i) for i in devices if i - distance in devices]
    return lax.ppermute(block, axis, route)


def time_features(timestep, embed_width):
    half_width = embed_width // 2
    freqs = jnp.exp(-math.log(10000.0) * jnp.arange(half_width, dtype=jnp.float32) / half_width)
    angles = timestep[0].astype(jnp.float32) * freqs
    embed = jnp.concatenate([jnp.cos(angles), jnp.sin(angles)])
    return jax.nn.silu(embed).astype(jnp.bfloat16)


def ring_pieces(block, axis):
    size = lax.axis_size(axis)
    ring = size // 2
    position = lax.axis_index(axis)
    partner = lax.ppermute(block, axis, [(i, (i + ring) % size) for i in range(size)])
    pair = jnp.where(
        position // ring == 0, jnp.stack([block, partner]), jnp.stack([partner, block])
    )
    ring_pos = position % ring
    forward = [(y * ring + a, y * ring + (a + 1) % ring) for y in range(2) for a in range(ring)]
    backward = [(y * ring + a, y * ring + (a - 1) % ring) for y in range(2) for a in range(ring)]
    pieces = [(pair, ring_pos)]
    ahead = pair
    behind = pair
    for step in range(1, ring // 2 + 1):
        ahead = lax.ppermute(ahead, axis, forward)
        pieces.append((ahead, (ring_pos - step) % ring))
        if step < ring - ring // 2:
            behind = lax.ppermute(behind, axis, backward)
            pieces.append((behind, (ring_pos + step) % ring))
    return pieces, ring


def ring_gather(block, axis):
    pieces, ring = ring_pieces(block, axis)
    gathered = jnp.zeros((ring,) + pieces[0][0].shape, block.dtype)
    for piece, source in pieces:
        gathered = lax.dynamic_update_index_in_dim(gathered, piece, source, 0)
    gathered = jnp.swapaxes(gathered, 0, 1)
    return gathered.reshape((2 * ring * block.shape[0],) + block.shape[1:])


def halving_scatter(partial, axis, order):
    size = lax.axis_size(axis)
    position = lax.axis_index(axis)
    state = partial
    for bit in order:
        half = state.shape[1] // 2
        mine = (position >> bit) & 1
        keep = lax.dynamic_slice_in_dim(state, mine * half, half, 1)
        send = lax.dynamic_slice_in_dim(state, (1 - mine) * half, half, 1)
        got = lax.ppermute(
            send.astype(jnp.bfloat16), axis, [(i, i ^ (1 << bit)) for i in range(size)]
        )
        state = keep + got.astype(jnp.float32)
    return state


def attend_piece(state_now, kv_piece, key_frame, queries, query_frame, query_first, head_dim):
    run_max, run_sum, accumulated = state_now
    key_part = kv_piece[:, :, :head_dim]
    value_part = kv_piece[:, :, head_dim:]
    scores = jnp.einsum(
        "nhe,mhe->nhm", queries, key_part, preferred_element_type=jnp.float32
    ) * head_dim ** (-0.5)
    allowed = (key_frame[None, :] <= query_frame[:, None]) & (
        key_frame[None, :] >= query_first[:, None]
    )
    masked = jnp.where(allowed[:, None, :], scores, NEG)
    new_max = jnp.maximum(run_max, masked.max(-1))
    exponent = jnp.where(allowed[:, None, :], jnp.exp(masked - new_max[..., None]), 0.0)
    factor = jnp.exp(run_max - new_max)
    run_sum = run_sum * factor + exponent.sum(-1)
    accumulated = accumulated * factor[..., None] + jnp.einsum(
        "nhm,mhe->nhe",
        exponent.astype(jnp.bfloat16),
        value_part,
        preferred_element_type=jnp.float32,
    )
    return (new_max, run_sum, accumulated)


def per_device(
    latents, timestep, offsets, qkv_weight, mod_weight, gate_weight, out_weight, conv_weight
):
    tok_rows = latents.shape[0]
    heads_here = qkv_weight.shape[1]
    head_dim = out_weight.shape[2]
    chan_here = gate_weight.shape[1]
    frame_size = HH * WW
    frames_here = tok_rows // frame_size
    position = lax.axis_index("ctx")
    column = lax.axis_index("fsdp")
    time_act = time_features(timestep, gate_weight.shape[0])
    gate_vec = jnp.dot(time_act, gate_weight, preferred_element_type=jnp.float32)
    float_rows = latents.astype(jnp.float32)
    centred = float_rows - float_rows.mean(-1, keepdims=True)
    variance = (centred * centred).mean(-1, keepdims=True)
    normed = centred * lax.rsqrt(variance + EPS)

    rows_here = qkv_weight.shape[0]
    qkv_width = qkv_weight.shape[2]
    qkv_cols = heads_here * qkv_width
    out_cols = heads_here * head_dim
    width = qkv_cols + out_cols
    local_shares = jnp.einsum(
        "rjt,t->rj", mod_weight, time_act, preferred_element_type=jnp.float32
    )
    shares_hi = local_shares.astype(jnp.bfloat16)
    shares_lo = (local_shares - shares_hi.astype(jnp.float32)).astype(jnp.bfloat16)
    share_count = 4 * rows_here
    extra_rows = 8 * ((share_count + 8 * width - 1) // (8 * width))
    share_block = jnp.zeros((extra_rows * width,), jnp.bfloat16)
    share_block = share_block.at[:share_count].set(
        jnp.concatenate([shares_hi, shares_lo], axis=1).reshape(share_count)
    )
    bundle = jnp.concatenate(
        [
            jnp.concatenate(
                [
                    qkv_weight.reshape(rows_here, qkv_cols),
                    out_weight.reshape(rows_here, out_cols),
                ],
                axis=1,
            ),
            share_block.reshape(extra_rows, width),
        ],
        axis=0,
    )
    gathered = ring_gather(bundle, "ctx")
    blocks = gathered.shape[0] // bundle.shape[0]
    gathered = gathered.reshape(blocks, rows_here + extra_rows, width)
    full_rows = blocks * rows_here
    w_piece = gathered[:, :rows_here, :qkv_cols].reshape(full_rows, heads_here, qkv_width)
    o_piece = gathered[:, :rows_here, qkv_cols:].reshape(full_rows, heads_here, head_dim)
    share_bits = (
        gathered[:, rows_here:, :]
        .reshape(blocks, extra_rows * width)[:, :share_count]
        .reshape(full_rows, 4)
        .astype(jnp.float32)
    )
    shares = share_bits[:, :2] + share_bits[:, 2:]

    modulated = (normed * (1.0 + shares[:, 1]) + shares[:, 0]).astype(jnp.bfloat16)
    projected_qkv = jnp.einsum(
        "nr,rhc->nhc", modulated, w_piece, preferred_element_type=jnp.float32
    ).astype(jnp.bfloat16)
    queries = projected_qkv[:, :, :head_dim]
    packed = projected_qkv[:, :, head_dim:]
    query_frame = position * frames_here + jnp.arange(tok_rows, dtype=jnp.int32) // frame_size
    local_first = lax.dynamic_slice_in_dim(offsets, position * frames_here, frames_here, 0)
    query_first = jnp.repeat(local_first, frame_size)
    state = (
        jnp.full((tok_rows, heads_here), NEG, jnp.float32),
        jnp.zeros((tok_rows, heads_here), jnp.float32),
        jnp.zeros((tok_rows, heads_here, head_dim), jnp.float32),
    )
    size = lax.axis_size("ctx")
    ring = size // 2
    partner = lax.ppermute(packed, "ctx", [(i, (i + ring) % size) for i in range(size)])
    pair = jnp.where(
        position // ring == 0, jnp.stack([packed, partner]), jnp.stack([partner, packed])
    )
    ring_pos = position % ring
    forward = [(y * ring + a, y * ring + (a + 1) % ring) for y in range(2) for a in range(ring)]
    backward = [(y * ring + a, y * ring + (a - 1) % ring) for y in range(2) for a in range(ring)]
    token_ids = jnp.arange(tok_rows, dtype=jnp.int32)

    frame_pattern = jnp.concatenate([token_ids, ring * tok_rows + token_ids]) // frame_size

    def fold(state_in, piece, source):
        key_frame = source * frames_here + frame_pattern
        return attend_piece(
            state_in,
            piece.reshape((2 * tok_rows,) + piece.shape[2:]),
            key_frame,
            queries,
            query_frame,
            query_first,
            head_dim,
        )

    ahead = pair
    behind = pair
    waiting = [(pair, ring_pos)]
    for step in range(1, ring // 2 + 1):
        ahead, state = lax.optimization_barrier((ahead, state))
        ahead = lax.ppermute(ahead, "ctx", forward)
        arrived = [(ahead, (ring_pos - step) % ring)]
        if step < ring - ring // 2:
            behind = lax.ppermute(behind, "ctx", backward)
            arrived.append((behind, (ring_pos + step) % ring))
        for piece, source in waiting:
            state = fold(state, piece, source)
        waiting = arrived
    for piece, source in waiting:
        state = fold(state, piece, source)
    run_max, run_sum, accumulated = state
    attended = (accumulated / run_sum[..., None]).astype(jnp.bfloat16)
    size = lax.axis_size("fsdp")
    bits = size.bit_length() - 1
    middle = list(range(1, bits - 1))
    half_rows = tok_rows // 2
    orders = [[0, bits - 1] + middle, [0] + middle + [bits - 1]]
    head_parts = []
    for part, order in enumerate(orders):
        by_bit = o_piece.reshape((2,) * bits + (full_rows // size,) + o_piece.shape[1:])
        permuted = jnp.transpose(
            by_bit,
            [bits - 1 - bit for bit in order] + list(range(bits, by_bit.ndim)),
        )
        partial_out = jnp.einsum(
            "nhe,rhe->nr",
            attended[part * half_rows : (part + 1) * half_rows],
            permuted.reshape(o_piece.shape),
            preferred_element_type=jnp.float32,
        )
        head_parts.append(halving_scatter(partial_out, "fsdp", order))
    head_total = jnp.concatenate(head_parts, axis=0)
    own_chan = lax.dynamic_slice_in_dim(latents, column * chan_here, chan_here, 1)
    before = passed_along(own_chan, "ctx", 1)
    stacked = (
        jnp.concatenate([before, own_chan], 0)
        .astype(jnp.float32)
        .reshape(frames_here + 2, HH, WW, chan_here)
    )
    padded = jnp.pad(stacked, ((0, 0), (1, 1), (1, 1), (0, 0)))
    convolved = jnp.zeros((frames_here, HH, WW, chan_here), jnp.float32)
    for time_lag in range(3):
        for row_shift in range(3):
            for col_shift in range(3):
                tap = conv_weight[time_lag, row_shift, col_shift].astype(jnp.float32)
                convolved = (
                    convolved
                    + tap
                    * padded[
                        2 - time_lag : 2 - time_lag + frames_here,
                        row_shift : row_shift + HH,
                        col_shift : col_shift + WW,
                    ]
                )
    residual = own_chan.astype(jnp.float32)
    mixed = residual + gate_vec * head_total + convolved.reshape(tok_rows, chan_here)
    return mixed.astype(jnp.bfloat16)


def solution(mesh):
    in_specs = (
        P("ctx", None),
        P(),
        P(),
        P("ctx", "fsdp", None),
        P("ctx", None, None),
        P(None, "fsdp"),
        P("ctx", "fsdp", None),
        P(None, None, None, "fsdp"),
    )
    out_specs = P("ctx", "fsdp")
    return jax.shard_map(
        per_device, mesh=mesh, in_specs=in_specs, out_specs=out_specs, check_vma=False
    )
```

```python
import math

import jax
import jax.numpy as jnp
from jax import lax
from jax.sharding import PartitionSpec as P

HH = 10
WW = 16


EPS = 1e-06
NEG = -1e30


def passed_along(block, axis, distance):
    devices = range(lax.axis_size(axis))
    route = [(i - distance, i) for i in devices if i - distance in devices]
    return lax.ppermute(block, axis, route)


def time_features(timestep, embed_width):
    half_width = embed_width // 2
    freqs = jnp.exp(-math.log(10000.0) * jnp.arange(half_width, dtype=jnp.float32) / half_width)
    angles = timestep[0].astype(jnp.float32) * freqs
    embed = jnp.concatenate([jnp.cos(angles), jnp.sin(angles)])
    return jax.nn.silu(embed).astype(jnp.bfloat16)


def ring_pieces(block, axis):
    size = lax.axis_size(axis)
    ring = size // 2
    position = lax.axis_index(axis)
    partner = lax.ppermute(block, axis, [(i, (i + ring) % size) for i in range(size)])
    pair = jnp.where(
        position // ring == 0, jnp.stack([block, partner]), jnp.stack([partner, block])
    )
    ring_pos = position % ring
    forward = [(y * ring + a, y * ring + (a + 1) % ring) for y in range(2) for a in range(ring)]
    backward = [(y * ring + a, y * ring + (a - 1) % ring) for y in range(2) for a in range(ring)]
    pieces = [(pair, ring_pos)]
    ahead = pair
    behind = pair
    for step in range(1, ring // 2 + 1):
        ahead = lax.ppermute(ahead, axis, forward)
        pieces.append((ahead, (ring_pos - step) % ring))
        if step < ring - ring // 2:
            behind = lax.ppermute(behind, axis, backward)
            pieces.append((behind, (ring_pos + step) % ring))
    return pieces, ring


def ring_gather(block, axis):
    pieces, ring = ring_pieces(block, axis)
    gathered = jnp.zeros((ring,) + pieces[0][0].shape, block.dtype)
    for piece, source in pieces:
        gathered = lax.dynamic_update_index_in_dim(gathered, piece, source, 0)
    return gathered


def halving_scatter(partial, axis, order):
    size = lax.axis_size(axis)
    position = lax.axis_index(axis)
    state = partial
    for bit in order:
        half = state.shape[1] // 2
        mine = (position >> bit) & 1
        keep = lax.dynamic_slice_in_dim(state, mine * half, half, 1)
        send = lax.dynamic_slice_in_dim(state, (1 - mine) * half, half, 1)
        got = lax.ppermute(
            send.astype(jnp.bfloat16), axis, [(i, i ^ (1 << bit)) for i in range(size)]
        )
        state = keep + got.astype(jnp.float32)
    return state


def attend_piece(state_now, kv_piece, key_frame, queries, query_frame, query_first, head_dim):
    run_max, run_sum, accumulated = state_now
    key_part = kv_piece[:, :, :head_dim]
    value_part = kv_piece[:, :, head_dim:]
    scores = jnp.einsum(
        "nhe,mhe->nhm", queries, key_part, preferred_element_type=jnp.float32
    ) * head_dim ** (-0.5)
    allowed = (key_frame[None, :] <= query_frame[:, None]) & (
        key_frame[None, :] >= query_first[:, None]
    )
    masked = jnp.where(allowed[:, None, :], scores, NEG)
    new_max = jnp.maximum(run_max, masked.max(-1))
    exponent = jnp.where(allowed[:, None, :], jnp.exp(masked - new_max[..., None]), 0.0)
    factor = jnp.exp(run_max - new_max)
    run_sum = run_sum * factor + exponent.sum(-1)
    accumulated = accumulated * factor[..., None] + jnp.einsum(
        "nhm,mhe->nhe",
        exponent.astype(jnp.bfloat16),
        value_part,
        preferred_element_type=jnp.float32,
    )
    return (new_max, run_sum, accumulated)


def per_device(
    latents, timestep, offsets, qkv_weight, mod_weight, gate_weight, out_weight, conv_weight
):
    tok_rows = latents.shape[0]
    heads_here = qkv_weight.shape[1]
    head_dim = out_weight.shape[2]
    chan_here = gate_weight.shape[1]
    frame_size = HH * WW
    frames_here = tok_rows // frame_size
    position = lax.axis_index("ctx")
    column = lax.axis_index("fsdp")
    time_act = time_features(timestep, gate_weight.shape[0])
    gate_vec = jnp.dot(time_act, gate_weight, preferred_element_type=jnp.float32)
    float_rows = latents.astype(jnp.float32)
    centred = float_rows - float_rows.mean(-1, keepdims=True)
    variance = (centred * centred).mean(-1, keepdims=True)
    normed = centred * lax.rsqrt(variance + EPS)

    rows_here = qkv_weight.shape[0]
    qkv_width = qkv_weight.shape[2]
    qkv_cols = heads_here * qkv_width
    out_cols = heads_here * head_dim
    width = qkv_cols + out_cols
    local_shares = jnp.einsum(
        "rjt,t->rj", mod_weight, time_act, preferred_element_type=jnp.float32
    )
    shares_hi = local_shares.astype(jnp.bfloat16)
    shares_lo = (local_shares - shares_hi.astype(jnp.float32)).astype(jnp.bfloat16)
    share_count = 4 * rows_here
    extra_rows = 8 * ((share_count + 8 * width - 1) // (8 * width))
    share_block = jnp.zeros((extra_rows * width,), jnp.bfloat16)
    share_block = share_block.at[:share_count].set(
        jnp.concatenate([shares_hi, shares_lo], axis=1).reshape(share_count)
    )
    bundle = jnp.concatenate(
        [
            jnp.concatenate(
                [
                    qkv_weight.reshape(rows_here, qkv_cols),
                    out_weight.reshape(rows_here, out_cols),
                ],
                axis=1,
            ),
            share_block.reshape(extra_rows, width),
        ],
        axis=0,
    )
    stacked_blocks = ring_gather(bundle, "ctx")
    ring = stacked_blocks.shape[0]
    block_rows = rows_here + extra_rows
    blocks = 2 * ring
    gathered = jnp.swapaxes(stacked_blocks, 0, 1).reshape(blocks, block_rows, width)
    full_rows = blocks * rows_here
    o_piece = gathered[:, :rows_here, qkv_cols:].reshape(full_rows, heads_here, head_dim)
    share_bits = (
        stacked_blocks[:, :, rows_here:, :]
        .reshape(ring, 2, extra_rows * width)[:, :, :share_count]
        .reshape(ring, 2, rows_here, 4)
        .astype(jnp.float32)
    )
    shares = share_bits[..., :2] + share_bits[..., 2:]
    normed_blocks = jnp.swapaxes(normed.reshape(tok_rows, 2, ring, rows_here), 1, 2)
    modulated = (normed_blocks * (1.0 + shares[..., 1]) + shares[..., 0]).astype(jnp.bfloat16)
    modulated = jnp.pad(modulated, ((0, 0), (0, 0), (0, 0), (0, extra_rows)))
    projected_all = jnp.dot(
        modulated.reshape(tok_rows, ring * 2 * block_rows),
        stacked_blocks.reshape(ring * 2 * block_rows, width),
        preferred_element_type=jnp.float32,
    )
    projected_qkv = (
        projected_all[:, :qkv_cols].astype(jnp.bfloat16).reshape(tok_rows, heads_here, qkv_width)
    )
    queries = projected_qkv[:, :, :head_dim]
    packed = projected_qkv[:, :, head_dim:]
    query_frame = position * frames_here + jnp.arange(tok_rows, dtype=jnp.int32) // frame_size
    local_first = lax.dynamic_slice_in_dim(offsets, position * frames_here, frames_here, 0)
    query_first = jnp.repeat(local_first, frame_size)
    state = (
        jnp.full((tok_rows, heads_here), NEG, jnp.float32),
        jnp.zeros((tok_rows, heads_here), jnp.float32),
        jnp.zeros((tok_rows, heads_here, head_dim), jnp.float32),
    )
    size = lax.axis_size("ctx")
    ring = size // 2
    partner = lax.ppermute(packed, "ctx", [(i, (i + ring) % size) for i in range(size)])
    pair = jnp.where(
        position // ring == 0, jnp.stack([packed, partner]), jnp.stack([partner, packed])
    )
    ring_pos = position % ring
    forward = [(y * ring + a, y * ring + (a + 1) % ring) for y in range(2) for a in range(ring)]
    backward = [(y * ring + a, y * ring + (a - 1) % ring) for y in range(2) for a in range(ring)]
    token_ids = jnp.arange(tok_rows, dtype=jnp.int32)

    frame_pattern = jnp.concatenate([token_ids, ring * tok_rows + token_ids]) // frame_size

    def fold(state_in, piece, source):
        key_frame = source * frames_here + frame_pattern
        return attend_piece(
            state_in,
            piece.reshape((2 * tok_rows,) + piece.shape[2:]),
            key_frame,
            queries,
            query_frame,
            query_first,
            head_dim,
        )

    ahead = pair
    behind = pair
    waiting = [(pair, ring_pos)]
    for step in range(1, ring // 2 + 1):
        ahead, state = lax.optimization_barrier((ahead, state))
        ahead = lax.ppermute(ahead, "ctx", forward)
        arrived = [(ahead, (ring_pos - step) % ring)]
        if step < ring - ring // 2:
            behind = lax.ppermute(behind, "ctx", backward)
            arrived.append((behind, (ring_pos + step) % ring))
        for piece, source in waiting:
            state = fold(state, piece, source)
        waiting = arrived
    for piece, source in waiting:
        state = fold(state, piece, source)
    run_max, run_sum, accumulated = state
    attended = (accumulated / run_sum[..., None]).astype(jnp.bfloat16)
    size = lax.axis_size("fsdp")
    bits = size.bit_length() - 1
    middle = list(range(1, bits - 1))
    half_rows = tok_rows // 2
    orders = [[0, bits - 1] + middle, [0] + middle + [bits - 1]]
    head_parts = []
    for part, order in enumerate(orders):
        by_bit = o_piece.reshape((2,) * bits + (full_rows // size,) + o_piece.shape[1:])
        permuted = jnp.transpose(
            by_bit,
            [bits - 1 - bit for bit in order] + list(range(bits, by_bit.ndim)),
        )
        partial_out = jnp.einsum(
            "nhe,rhe->nr",
            attended[part * half_rows : (part + 1) * half_rows],
            permuted.reshape(o_piece.shape),
            preferred_element_type=jnp.float32,
        )
        head_parts.append(halving_scatter(partial_out, "fsdp", order))
    head_total = jnp.concatenate(head_parts, axis=0)
    own_chan = lax.dynamic_slice_in_dim(latents, column * chan_here, chan_here, 1)
    before = passed_along(own_chan, "ctx", 1)
    stacked = (
        jnp.concatenate([before, own_chan], 0)
        .astype(jnp.float32)
        .reshape(frames_here + 2, HH, WW, chan_here)
    )
    padded = jnp.pad(stacked, ((0, 0), (1, 1), (1, 1), (0, 0)))
    convolved = jnp.zeros((frames_here, HH, WW, chan_here), jnp.float32)
    for time_lag in range(3):
        for row_shift in range(3):
            for col_shift in range(3):
                tap = conv_weight[time_lag, row_shift, col_shift].astype(jnp.float32)
                convolved = (
                    convolved
                    + tap
                    * padded[
                        2 - time_lag : 2 - time_lag + frames_here,
                        row_shift : row_shift + HH,
                        col_shift : col_shift + WW,
                    ]
                )
    residual = own_chan.astype(jnp.float32)
    mixed = residual + gate_vec * head_total + convolved.reshape(tok_rows, chan_here)
    return mixed.astype(jnp.bfloat16)


def solution(mesh):
    in_specs = (
        P("ctx", None),
        P(),
        P(),
        P("ctx", "fsdp", None),
        P("ctx", None, None),
        P(None, "fsdp"),
        P("ctx", "fsdp", None),
        P(None, None, None, "fsdp"),
    )
    out_specs = P("ctx", "fsdp")
    return jax.shard_map(
        per_device, mesh=mesh, in_specs=in_specs, out_specs=out_specs, check_vma=False
    )
```

```python
import math

import jax
import jax.numpy as jnp
from jax import lax
from jax.sharding import PartitionSpec as P

HH = 10
WW = 16


EPS = 1e-06
NEG = -1e30


def passed_along(block, axis, distance):
    devices = range(lax.axis_size(axis))
    route = [(i - distance, i) for i in devices if i - distance in devices]
    return lax.ppermute(block, axis, route)


def time_features(timestep, embed_width):
    half_width = embed_width // 2
    freqs = jnp.exp(-math.log(10000.0) * jnp.arange(half_width, dtype=jnp.float32) / half_width)
    angles = timestep[0].astype(jnp.float32) * freqs
    embed = jnp.concatenate([jnp.cos(angles), jnp.sin(angles)])
    return jax.nn.silu(embed).astype(jnp.bfloat16)


def ring_pieces(block, axis):
    size = lax.axis_size(axis)
    ring = size // 2
    position = lax.axis_index(axis)
    partner = lax.ppermute(block, axis, [(i, (i + ring) % size) for i in range(size)])
    pair = jnp.where(
        position // ring == 0, jnp.stack([block, partner]), jnp.stack([partner, block])
    )
    ring_pos = position % ring
    forward = [(y * ring + a, y * ring + (a + 1) % ring) for y in range(2) for a in range(ring)]
    backward = [(y * ring + a, y * ring + (a - 1) % ring) for y in range(2) for a in range(ring)]
    pieces = [(pair, ring_pos)]
    ahead = pair
    behind = pair
    for step in range(1, ring // 2 + 1):
        ahead = lax.ppermute(ahead, axis, forward)
        pieces.append((ahead, (ring_pos - step) % ring))
        if step < ring - ring // 2:
            behind = lax.ppermute(behind, axis, backward)
            pieces.append((behind, (ring_pos + step) % ring))
    return pieces, ring


def ring_gather(block, axis):
    pieces, ring = ring_pieces(block, axis)
    gathered = jnp.zeros((ring,) + pieces[0][0].shape, block.dtype)
    for piece, source in pieces:
        gathered = lax.dynamic_update_index_in_dim(gathered, piece, source, 0)
    gathered = jnp.swapaxes(gathered, 0, 1)
    return gathered.reshape((2 * ring * block.shape[0],) + block.shape[1:])


def halving_scatter(partial, axis, order):
    size = lax.axis_size(axis)
    position = lax.axis_index(axis)
    state = partial
    for bit in order:
        half = state.shape[1] // 2
        mine = (position >> bit) & 1
        keep = lax.dynamic_slice_in_dim(state, mine * half, half, 1)
        send = lax.dynamic_slice_in_dim(state, (1 - mine) * half, half, 1)
        got = lax.ppermute(
            send.astype(jnp.bfloat16), axis, [(i, i ^ (1 << bit)) for i in range(size)]
        )
        state = keep + got.astype(jnp.float32)
    return state


def attend_piece(state_now, kv_piece, key_frame, queries, query_frame, query_first, head_dim):
    run_max, run_sum, accumulated = state_now
    key_part = kv_piece[:, :, :head_dim]
    value_part = kv_piece[:, :, head_dim:]
    scores = jnp.einsum(
        "nhe,mhe->nhm", queries, key_part, preferred_element_type=jnp.float32
    ) * head_dim ** (-0.5)
    allowed = (key_frame[None, :] <= query_frame[:, None]) & (
        key_frame[None, :] >= query_first[:, None]
    )
    masked = jnp.where(allowed[:, None, :], scores, NEG)
    new_max = jnp.maximum(run_max, masked.max(-1))
    exponent = jnp.where(allowed[:, None, :], jnp.exp(masked - new_max[..., None]), 0.0)
    factor = jnp.exp(run_max - new_max)
    run_sum = run_sum * factor + exponent.sum(-1)
    accumulated = accumulated * factor[..., None] + jnp.einsum(
        "nhm,mhe->nhe",
        exponent.astype(jnp.bfloat16),
        value_part,
        preferred_element_type=jnp.float32,
    )
    return (new_max, run_sum, accumulated)


def per_device(
    latents, timestep, offsets, qkv_weight, mod_weight, gate_weight, out_weight, conv_weight
):
    tok_rows = latents.shape[0]
    heads_here = qkv_weight.shape[1]
    head_dim = out_weight.shape[2]
    chan_here = gate_weight.shape[1]
    frame_size = HH * WW
    frames_here = tok_rows // frame_size
    position = lax.axis_index("ctx")
    column = lax.axis_index("fsdp")
    time_act = time_features(timestep, gate_weight.shape[0])
    gate_vec = jnp.dot(time_act, gate_weight, preferred_element_type=jnp.float32)
    float_rows = latents.astype(jnp.float32)
    centred = float_rows - float_rows.mean(-1, keepdims=True)
    variance = (centred * centred).mean(-1, keepdims=True)
    normed = centred * lax.rsqrt(variance + EPS)

    rows_here = qkv_weight.shape[0]
    qkv_width = qkv_weight.shape[2]
    qkv_cols = heads_here * qkv_width
    out_cols = heads_here * head_dim
    width = qkv_cols + out_cols
    local_shares = jnp.einsum(
        "rjt,t->rj", mod_weight, time_act, preferred_element_type=jnp.float32
    )
    shares_hi = local_shares.astype(jnp.bfloat16)
    shares_lo = (local_shares - shares_hi.astype(jnp.float32)).astype(jnp.bfloat16)
    share_count = 4 * rows_here
    extra_rows = 8 * ((share_count + 8 * width - 1) // (8 * width))
    share_block = jnp.zeros((extra_rows * width,), jnp.bfloat16)
    share_block = share_block.at[:share_count].set(
        jnp.concatenate([shares_hi, shares_lo], axis=1).reshape(share_count)
    )
    bundle = jnp.concatenate(
        [
            jnp.concatenate(
                [
                    qkv_weight.reshape(rows_here, qkv_cols),
                    out_weight.reshape(rows_here, out_cols),
                ],
                axis=1,
            ),
            share_block.reshape(extra_rows, width),
        ],
        axis=0,
    )
    gathered = ring_gather(bundle, "ctx")
    blocks = gathered.shape[0] // bundle.shape[0]
    gathered = gathered.reshape(blocks, rows_here + extra_rows, width)
    full_rows = blocks * rows_here
    w_piece = gathered[:, :rows_here, :qkv_cols].reshape(full_rows, heads_here, qkv_width)
    o_piece = gathered[:, :rows_here, qkv_cols:].reshape(full_rows, heads_here, head_dim)
    share_bits = (
        gathered[:, rows_here:, :]
        .reshape(blocks, extra_rows * width)[:, :share_count]
        .reshape(full_rows, 4)
        .astype(jnp.float32)
    )
    shares = share_bits[:, :2] + share_bits[:, 2:]

    modulated = (normed * (1.0 + shares[:, 1]) + shares[:, 0]).astype(jnp.bfloat16)
    projected_qkv = jnp.einsum(
        "nr,rhc->nhc", modulated, w_piece, preferred_element_type=jnp.float32
    ).astype(jnp.bfloat16)
    queries = projected_qkv[:, :, :head_dim]
    packed = projected_qkv[:, :, head_dim:]
    query_frame = position * frames_here + jnp.arange(tok_rows, dtype=jnp.int32) // frame_size
    local_first = lax.dynamic_slice_in_dim(offsets, position * frames_here, frames_here, 0)
    query_first = jnp.repeat(local_first, frame_size)
    state = (
        jnp.full((tok_rows, heads_here), NEG, jnp.float32),
        jnp.zeros((tok_rows, heads_here), jnp.float32),
        jnp.zeros((tok_rows, heads_here, head_dim), jnp.float32),
    )
    size = lax.axis_size("ctx")
    ring = size // 2
    partner = lax.ppermute(packed, "ctx", [(i, (i + ring) % size) for i in range(size)])
    pair = jnp.where(
        position // ring == 0, jnp.stack([packed, partner]), jnp.stack([partner, packed])
    )
    ring_pos = position % ring
    forward = [(y * ring + a, y * ring + (a + 1) % ring) for y in range(2) for a in range(ring)]
    backward = [(y * ring + a, y * ring + (a - 1) % ring) for y in range(2) for a in range(ring)]
    token_ids = jnp.arange(tok_rows, dtype=jnp.int32)

    frame_pattern = jnp.concatenate([token_ids, ring * tok_rows + token_ids]) // frame_size

    def fold(state_in, piece, source):
        key_frame = source * frames_here + frame_pattern
        return attend_piece(
            state_in,
            piece.reshape((2 * tok_rows,) + piece.shape[2:]),
            key_frame,
            queries,
            query_frame,
            query_first,
            head_dim,
        )

    ahead = pair
    behind = pair
    waiting = [(pair, ring_pos)]
    for step in range(1, ring // 2 + 1):
        ahead, state = lax.optimization_barrier((ahead, state))
        ahead = lax.ppermute(ahead, "ctx", forward)
        arrived = [(ahead, (ring_pos - step) % ring)]
        if step < ring - ring // 2:
            behind = lax.ppermute(behind, "ctx", backward)
            arrived.append((behind, (ring_pos + step) % ring))
        for piece, source in waiting:
            state = fold(state, piece, source)
        waiting = arrived
    for piece, source in waiting:
        state = fold(state, piece, source)
    run_max, run_sum, accumulated = state
    attended = (accumulated / run_sum[..., None]).astype(jnp.bfloat16)
    size = lax.axis_size("fsdp")
    bits = size.bit_length() - 1
    middle = list(range(1, bits - 1))
    half_rows = tok_rows // 2
    orders = [[0, bits - 1] + middle, [0] + middle[:1] + [bits - 1] + middle[1:]]
    head_parts = []
    for part, order in enumerate(orders):
        by_bit = o_piece.reshape((2,) * bits + (full_rows // size,) + o_piece.shape[1:])
        permuted = jnp.transpose(
            by_bit,
            [bits - 1 - bit for bit in order] + list(range(bits, by_bit.ndim)),
        )
        partial_out = jnp.einsum(
            "nhe,rhe->nr",
            attended[part * half_rows : (part + 1) * half_rows],
            permuted.reshape(o_piece.shape),
            preferred_element_type=jnp.float32,
        )
        head_parts.append(halving_scatter(partial_out, "fsdp", order))
    head_total = jnp.concatenate(head_parts, axis=0)
    own_chan = lax.dynamic_slice_in_dim(latents, column * chan_here, chan_here, 1)
    before = passed_along(own_chan, "ctx", 1)
    stacked = (
        jnp.concatenate([before, own_chan], 0)
        .astype(jnp.float32)
        .reshape(frames_here + 2, HH, WW, chan_here)
    )
    padded = jnp.pad(stacked, ((0, 0), (1, 1), (1, 1), (0, 0)))
    convolved = jnp.zeros((frames_here, HH, WW, chan_here), jnp.float32)
    for time_lag in range(3):
        for row_shift in range(3):
            for col_shift in range(3):
                tap = conv_weight[time_lag, row_shift, col_shift].astype(jnp.float32)
                convolved = (
                    convolved
                    + tap
                    * padded[
                        2 - time_lag : 2 - time_lag + frames_here,
                        row_shift : row_shift + HH,
                        col_shift : col_shift + WW,
                    ]
                )
    residual = own_chan.astype(jnp.float32)
    mixed = residual + gate_vec * head_total + convolved.reshape(tok_rows, chan_here)
    return mixed.astype(jnp.bfloat16)


def solution(mesh):
    in_specs = (
        P("ctx", None),
        P(),
        P(),
        P("ctx", "fsdp", None),
        P("ctx", None, None),
        P(None, "fsdp"),
        P("ctx", "fsdp", None),
        P(None, None, None, "fsdp"),
    )
    out_specs = P("ctx", "fsdp")
    return jax.shard_map(
        per_device, mesh=mesh, in_specs=in_specs, out_specs=out_specs, check_vma=False
    )
```
